256 devices in a mesh: pts: 128 (over y, z, x), rep: 2 (over core).
Axes of the slice: x: 4, y: 4, z: 8, core: 2. Of those that a mesh axis runs over, the one named last changes fastest.
Arguments:
- src_points: bfloat16 [393216, 256], P('pts'), may hold values from -7 to 7
- tgt_points: bfloat16 [393216, 256], P('pts'), may hold values from -7 to 7
- pair_source: int32 [24576], P(('pts', 'rep')), may hold values from -1 to 3071, as said below
- pair_target: int32 [24576], P(('pts', 'rep')), may hold values from -1 to 3071, as said below
- pair_count: int32 [256], P(('pts', 'rep')), may hold values from 12 to 96, as said below
Outputs:
- source_dual: float32 [393216], P('pts')
- target_dual: float32 [393216], P('pts')
- target_grad: float32 [393216, 256], P('pts')
The draws below stay inside these ranges and needn't reach their ends.
Inputs may be any that keep to these rules, and one draw needn't show every extreme that they name: `pair_source`: for the device at index d of pts+rep (pts index p = d // 2, rep index r = d % 2), the first pair_count[d] of its 96 slots name source blocks p * 24 to (p + 1) * 24 - 1; its other slots hold -1. `pair_target`: A listed target block t has owner t // 24; one device's listed slots name different owners, and only blocks whose index t % 24 lies in r * 12 to (r + 1) * 12 - 1; unlisted slots hold -1. No pair of blocks is listed twice; every source block and every target block is listed somewhere; some owner is named by every device. `pair_count`: some device lists 96 pairs.
All inputs are finite; a program needn't handle non-finite values.
Results may differ from the reference program's by a relative error of at most 0.0016.
Values may be sent and summed in bfloat16 or wider, within the bound.
No kernel may reach another device: no remote copies, remote signals or barrier semaphores. Data moves between devices by JAX's collectives and lax.ppermute only.
A program may use at most 192 MiB of HBM per device.

```python
import jax
import jax.numpy as jnp
from jax import lax

DIM = 256
BLOCK = 128
BLK_DEV = 24
TGT_MAX = 96
ITERS = 3
SLOTS_DEV = 96
BLOCKS = 3072
POINTS = 393216
SLOTS = 24576
N_PTS = 128
N_REP = 2


def point_cloud(key, salt):
    noise_key = jax.random.fold_in(jax.random.fold_in(key, salt), 0)
    point_rows = N_PTS * BLK_DEV * BLOCK
    return jnp.clip(jax.random.normal(noise_key, (point_rows, DIM), jnp.float32), -6.0, 6.0).astype(jnp.bfloat16)


def draw_src_points(key, part):
    return point_cloud(key, 3)


def draw_tgt_points(key, part):
    return point_cloud(key, 5)


def pair_tables(key):
    devices = N_PTS * N_REP
    half_blocks = BLK_DEV // N_REP
    most = min(TGT_MAX, N_PTS)
    spare = most - half_blocks - 1
    subkeys = [jax.random.fold_in(key, 100 + j) for j in range(8)]
    offsets = jax.random.permutation(subkeys[0], N_PTS)[:half_blocks]
    central = jax.random.randint(subkeys[1], (), 0, N_PTS)
    device_rank = jnp.arange(devices) // N_REP
    device_side = jnp.arange(devices) % N_REP
    fixed_owner = (device_rank[:, None] + offsets[None, :]) % N_PTS
    lanes = jnp.arange(N_PTS)
    taken = jnp.any(fixed_owner[:, :, None] == lanes[None, None, :], axis=1)
    central_fresh = jnp.logical_not(jnp.any(fixed_owner == central, axis=1))
    orders = jax.vmap(lambda sub: jax.random.permutation(sub, N_PTS))(jax.random.split(subkeys[2], devices))
    open_lane = jnp.logical_not(jnp.take_along_axis(taken, orders, axis=1)) & (orders != central)
    running = jnp.cumsum(open_lane.astype(jnp.int32), axis=1)
    first_draw = jax.random.randint(subkeys[3], (devices,), 0, spare + 1)
    second_draw = jax.random.randint(subkeys[4], (devices,), 0, spare + 1)
    wanted = first_draw * (2 * spare + second_draw) // (3 * spare)
    heavy = jax.random.randint(subkeys[5], (), 0, devices)
    wanted = jnp.where(jnp.arange(devices) == heavy, most - half_blocks - central_fresh.astype(jnp.int32), wanted)
    extra_live = open_lane & (running <= wanted[:, None])
    owners = jnp.concatenate([fixed_owner, jnp.full((devices, 1), central, jnp.int32), orders.astype(jnp.int32)], axis=1)
    live = jnp.concatenate([jnp.ones((devices, half_blocks), bool), central_fresh[:, None], extra_live], axis=1)
    span = half_blocks + 1 + N_PTS
    position = jnp.arange(span)[None, :]
    local_target = jnp.where(position < half_blocks, position, jax.random.randint(subkeys[6], (devices, span), 0, half_blocks))
    target_local = device_side[:, None] * half_blocks + local_target
    source_local = jnp.where(position < half_blocks, device_side[:, None] * half_blocks + position, jax.random.randint(subkeys[7], (devices, span), 0, BLK_DEV))
    ranking = jnp.argsort(jnp.where(live, 0, 1), axis=1, stable=True)[:, :most]
    listed_count = jnp.sum(live.astype(jnp.int32), axis=1)
    slot_live = jnp.arange(most)[None, :] < listed_count[:, None]
    owner_sel = jnp.take_along_axis(owners, ranking, axis=1)
    target_sel = jnp.take_along_axis(target_local, ranking, axis=1)
    source_sel = jnp.take_along_axis(source_local, ranking, axis=1)
    targets = jnp.where(slot_live, owner_sel * BLK_DEV + target_sel, -1).astype(jnp.int32)
    sources = jnp.where(slot_live, device_rank[:, None] * BLK_DEV + source_sel, -1).astype(jnp.int32)
    return (sources.reshape(-1), targets.reshape(-1), listed_count.astype(jnp.int32))


def draw_pair_source(key, part):
    return pair_tables(key)[0]


def draw_pair_target(key, part):
    return pair_tables(key)[1]


def draw_pair_count(key, part):
    return pair_tables(key)[2]


def setup_inputs(seed: int = 0) -> dict:
    splits = jax.random.split(jax.random.key(seed), 6)
    src_points = draw_src_points(jax.random.fold_in(splits[5], 71), 0)
    tgt_points = draw_tgt_points(jax.random.fold_in(splits[5], 71), 0)
    pair_source = draw_pair_source(jax.random.fold_in(splits[5], 71), 0)
    pair_target = draw_pair_target(jax.random.fold_in(splits[5], 71), 0)
    pair_count = draw_pair_count(jax.random.fold_in(splits[5], 71), 0)
    return {"src_points": src_points, "tgt_points": tgt_points, "pair_source": pair_source, "pair_target": pair_target, "pair_count": pair_count}


EPSILON = 0.05
NEG_BIG = -1.0e30


def pair_costs(source_rows, target_rows):
    xs = source_rows.astype(jnp.float32)
    ys = target_rows.astype(jnp.float32)
    inner_dot = jnp.einsum("gid,gjd->gij", xs, ys)
    source_sq = jnp.sum(xs * xs, axis=2)
    target_sq = jnp.sum(ys * ys, axis=2)
    return (source_sq[:, :, None] + target_sq[:, None, :] - 2.0 * inner_dot) / DIM


def settle(peaks, masses, block_key, listed):
    peaks = jnp.where(listed[:, None], peaks, NEG_BIG)
    masses = jnp.where(listed[:, None], masses, 0.0)
    maxima = jnp.full((BLOCKS, BLOCK), NEG_BIG, jnp.float32).at[block_key].max(peaks)
    totals = jnp.zeros((BLOCKS, BLOCK), jnp.float32).at[block_key].add(masses * jnp.exp(peaks - maxima[block_key]))
    return -EPSILON * (maxima + jnp.log(totals))


def reference(src_points, tgt_points, pair_source, pair_target, pair_count):
    source_blocks = src_points.reshape(BLOCKS, BLOCK, DIM)
    target_blocks = tgt_points.reshape(BLOCKS, BLOCK, DIM)
    slot_ids = jnp.arange(SLOTS, dtype=jnp.int32)
    listed = (slot_ids % SLOTS_DEV) < pair_count[slot_ids // SLOTS_DEV]
    source_ids = jnp.where(listed, pair_source, 0).astype(jnp.int32)
    target_ids = jnp.where(listed, pair_target, 0).astype(jnp.int32)
    groups = SLOTS // SLOTS_DEV
    source_groups = source_ids.reshape(groups, SLOTS_DEV)
    target_groups = target_ids.reshape(groups, SLOTS_DEV)
    listed_groups = listed.reshape(groups, SLOTS_DEV)

    def costs_of(group_no):
        return pair_costs(source_blocks[source_groups[group_no]], target_blocks[target_groups[group_no]])

    def row_update(target_dual):
        def one_group(group_no):
            scores = (target_dual[target_groups[group_no]][:, None, :] - costs_of(group_no)) / EPSILON
            peaks = jnp.max(scores, axis=2)
            return peaks, jnp.sum(jnp.exp(scores - peaks[:, :, None]), axis=2)

        peaks, masses = lax.map(one_group, jnp.arange(groups))
        return settle(peaks.reshape(SLOTS, BLOCK), masses.reshape(SLOTS, BLOCK), source_ids, listed)

    def column_update(source_dual):
        def one_group(group_no):
            scores = (source_dual[source_groups[group_no]][:, :, None] - costs_of(group_no)) / EPSILON
            peaks = jnp.max(scores, axis=1)
            return peaks, jnp.sum(jnp.exp(scores - peaks[:, None, :]), axis=1)

        peaks, masses = lax.map(one_group, jnp.arange(groups))
        return settle(peaks.reshape(SLOTS, BLOCK), masses.reshape(SLOTS, BLOCK), target_ids, listed)

    target_dual = jnp.zeros((BLOCKS, BLOCK), jnp.float32)
    source_dual = jnp.zeros((BLOCKS, BLOCK), jnp.float32)
    for round_no in range(ITERS):
        source_dual = row_update(target_dual)
        target_dual = column_update(source_dual)

    def gradient_step(carry, group_no):
        numerator, column_mass = carry
        plan = jnp.exp((source_dual[source_groups[group_no]][:, :, None] + target_dual[target_groups[group_no]][:, None, :] - costs_of(group_no)) / EPSILON)
        plan = jnp.where(listed_groups[group_no][:, None, None], plan, 0.0)
        weights = lax.optimization_barrier(plan.astype(jnp.bfloat16)).astype(jnp.float32)
        partial_value = jnp.einsum("gij,gid->gjd", weights, source_blocks[source_groups[group_no]].astype(jnp.float32))
        numerator = numerator.at[target_groups[group_no]].add(partial_value)
        column_mass = column_mass.at[target_groups[group_no]].add(jnp.sum(plan, axis=1))
        return (numerator, column_mass), None

    start = (jnp.zeros((BLOCKS, BLOCK, DIM), jnp.float32), jnp.zeros((BLOCKS, BLOCK), jnp.float32))
    (numerator, column_mass), unused = lax.scan(gradient_step, start, jnp.arange(groups))
    target_grad = target_blocks.astype(jnp.float32) * column_mass[:, :, None] - numerator
    return source_dual.reshape(POINTS), target_dual.reshape(POINTS), target_grad.reshape(POINTS, DIM)
```

```python
import jax
import jax.numpy as jnp
from jax import lax
from jax.sharding import PartitionSpec as P

BLOCK = 128
ITERS = 3


EPSILON = 0.05
NEG_BIG = -1e30


def squares(blocks_in):
    return jnp.sum(jnp.square(blocks_in.astype(jnp.float32)), axis=-1)


def pair_costs(source_rows, target_rows):
    inner_dot = jnp.einsum(
        "gid,gjd->gij", source_rows, target_rows, preferred_element_type=jnp.float32
    )
    source_sq = squares(source_rows)
    target_sq = squares(target_rows)
    return (source_sq[:, :, None] + target_sq[:, None, :] - 2.0 * inner_dot) / source_rows.shape[2]


def pair_lse(scores, axis):
    peaks = jnp.max(scores, axis=axis)
    masses = jnp.sum(jnp.exp(scores - jnp.expand_dims(peaks, axis)), axis=axis)
    return peaks + jnp.log(masses)


def combine_by(values, block_key, key_count):
    member = (block_key[:, None] == jnp.arange(key_count)[None, :])[:, :, None]
    maxima = jnp.max(jnp.where(member, values[:, None, :], NEG_BIG), axis=0)
    shifts = jnp.where(member, values[:, None, :] - maxima[None, :, :], NEG_BIG)
    totals = jnp.sum(jnp.where(member, jnp.exp(shifts), 0.0), axis=0)
    return maxima, totals


def swap_rep(value):
    return lax.ppermute(value, "rep", [(0, 1), (1, 0)])


def a2a(value):
    return lax.all_to_all(value, "pts", split_axis=0, concat_axis=0, tiled=True)


def on_device(src_points, tgt_points, pair_source, pair_target, pair_count):
    peer_count = lax.axis_size("pts")
    point_rows, feat_width = src_points.shape
    block_len = BLOCK
    blocks = point_rows // block_len
    half_blocks = blocks // lax.axis_size("rep")
    rep_index = lax.axis_index("rep")
    lower_block = rep_index * half_blocks
    own_sources = src_points.reshape(blocks, block_len, feat_width)
    own_targets = tgt_points.reshape(blocks, block_len, feat_width)

    pair_total = pair_count[0]
    slot_total = pair_source.shape[0]
    usable = jnp.arange(slot_total) < pair_total
    source_local = jnp.where(usable, pair_source % blocks, 0)
    owner_ids = jnp.where(usable, pair_target // blocks, 0)
    target_local = jnp.where(usable, pair_target % blocks, 0)
    matched = (owner_ids[:, None] == jnp.arange(peer_count)[None, :]) & usable[:, None]
    wanted = jnp.max(jnp.where(matched, target_local[:, None], -1), axis=0)
    source_of_owner = jnp.max(jnp.where(matched, source_local[:, None], -1), axis=0)
    served = source_of_owner >= 0
    source_index = jnp.maximum(source_of_owner, 0)
    outgoing = jnp.where(
        served[:, None, None], own_sources[source_index], jnp.zeros((), src_points.dtype)
    )
    asked_ids = a2a(wanted)
    received = a2a(outgoing)

    valid = asked_ids >= 0
    half_key = jnp.where(valid, asked_ids - lower_block, -1)
    half_pick = jnp.clip(half_key, 0, half_blocks - 1)
    own_half = lax.dynamic_slice_in_dim(own_targets, lower_block, half_blocks, 0)
    pair_targets = own_half[half_pick]
    cost_grid = pair_costs(received, pair_targets)

    target_half = jnp.zeros((half_blocks, block_len), jnp.float32)
    for round_no in range(ITERS):
        target_here = target_half[half_pick]
        row_lse = pair_lse((target_here[:, None, :] - cost_grid) / EPSILON, 2)
        row_back = a2a(row_lse)
        maxima, totals = combine_by(row_back, source_of_owner, blocks)
        other_maxima, other_totals = swap_rep((maxima, totals))
        merged = jnp.maximum(maxima, other_maxima)
        merged_totals = totals * jnp.exp(maxima - merged) + other_totals * jnp.exp(
            other_maxima - merged
        )
        source_dual = -EPSILON * (merged + jnp.log(merged_totals))
        sent_duals = jnp.where(served[:, None], source_dual[source_index], 0.0)
        source_here = a2a(sent_duals)
        column_lse = pair_lse((source_here[:, :, None] - cost_grid) / EPSILON, 1)
        col_max, col_tot = combine_by(column_lse, half_key, half_blocks)
        target_half = -EPSILON * (col_max + jnp.log(col_tot))

    target_here = target_half[half_pick]
    plan = jnp.exp((source_here[:, :, None] + target_here[:, None, :] - cost_grid) / EPSILON)
    plan = jnp.where(valid[:, None, None], plan, 0.0)
    partial_value = jnp.einsum(
        "gij,gid->gjd",
        plan.astype(jnp.bfloat16),
        received,
        preferred_element_type=jnp.float32,
    )
    member = (half_key[:, None] == jnp.arange(half_blocks)[None, :]).astype(jnp.float32)
    numerator = jnp.einsum("sb,sjd->bjd", member, partial_value, precision=lax.Precision.HIGHEST)
    column_mass = jnp.einsum(
        "sb,sj->bj", member, jnp.sum(plan, axis=1), precision=lax.Precision.HIGHEST
    )
    gradient_half = own_half.astype(jnp.float32) * column_mass[:, :, None] - numerator
    target_dual = lax.all_gather(target_half, "rep", axis=0, tiled=True)
    gradient = lax.all_gather(gradient_half, "rep", axis=0, tiled=True)
    return (
        source_dual.reshape(-1),
        target_dual.reshape(-1),
        gradient.reshape(blocks * block_len, feat_width),
    )


def solution(mesh):
    return jax.shard_map(
        on_device,
        mesh=mesh,
        in_specs=(
            P("pts", None),
            P("pts", None),
            P(("pts", "rep")),
            P(("pts", "rep")),
            P(("pts", "rep")),
        ),
        out_specs=(P("pts"), P("pts"), P("pts", None)),
        check_vma=False,
    )
```

```python
import functools

import jax
import jax.numpy as jnp
from jax import lax
from jax.experimental import pallas as pl
from jax.experimental.pallas import tpu as pltpu
from jax.sharding import PartitionSpec as P

BLOCK = 128
ITERS = 3


EPSILON = 0.05
NEG_BIG = -1e30
INV_EPS = 1.0 / EPSILON
PAIRS_STEP = 16


def as_column(row):
    side = row.shape[1]
    return jnp.transpose(jnp.broadcast_to(row, (side, side)))


def sweep_kernel(grid_ref, dual_ref, out_ref):
    def one(p, carry):
        dual_col = as_column(dual_ref[pl.ds(p, 1), :])
        scores = (dual_col - grid_ref[p]) * INV_EPS
        peak = jnp.max(scores, axis=0, keepdims=True)
        mass = jnp.sum(jnp.exp(scores - peak), axis=0, keepdims=True)
        out_ref[pl.ds(p, 1), :] = peak + jnp.log(mass)
        return carry

    lax.fori_loop(0, grid_ref.shape[0], one, 0)


def sweep(grids, duals):
    pairs, side, _ = grids.shape
    return pl.pallas_call(
        sweep_kernel,
        grid=(pairs // PAIRS_STEP,),
        in_specs=[
            pl.BlockSpec((PAIRS_STEP, side, side), lambda s: (s, 0, 0)),
            pl.BlockSpec((PAIRS_STEP, side), lambda s: (s, 0)),
        ],
        out_specs=pl.BlockSpec((PAIRS_STEP, side), lambda s: (s, 0)),
        out_shape=jax.ShapeDtypeStruct((pairs, side), jnp.float32),
        cost_estimate=pl.CostEstimate(
            flops=8 * pairs * side * side,
            transcendentals=pairs * side * side,
            bytes_accessed=4 * pairs * side * (side + 2),
        ),
    )(grids, duals)


def gradient_kernel(keys_ref, grid_t_ref, source_ref, target_ref, rows_ref, half_ref, out_ref):
    step = pl.program_id(0)

    @pl.when(step == 0)
    def _():
        out_ref[...] = jnp.zeros_like(out_ref)

    def one(p, carry):
        key = keys_ref[step * PAIRS_STEP + p]

        @pl.when(key >= 0)
        def _():
            target_col = as_column(target_ref[pl.ds(p, 1), :])
            plan_t = jnp.exp((source_ref[pl.ds(p, 1), :] + target_col - grid_t_ref[p]) * INV_EPS)
            mass = jnp.sum(plan_t, axis=1, keepdims=True)
            numerator = jnp.dot(
                plan_t.astype(jnp.bfloat16), rows_ref[p], preferred_element_type=jnp.float32
            )
            out_ref[key] += half_ref[key].astype(jnp.float32) * mass - numerator

        return carry

    lax.fori_loop(0, PAIRS_STEP, one, 0)


def gradient_sums(keys, grids_t, source_duals, target_duals, rows, half_targets):
    pairs, side, _ = grids_t.shape
    width = rows.shape[2]
    half = half_targets.shape[0]
    return pl.pallas_call(
        gradient_kernel,
        grid_spec=pltpu.PrefetchScalarGridSpec(
            num_scalar_prefetch=1,
            grid=(pairs // PAIRS_STEP,),
            in_specs=[
                pl.BlockSpec((PAIRS_STEP, side, side), lambda s, k: (s, 0, 0)),
                pl.BlockSpec((PAIRS_STEP, side), lambda s, k: (s, 0)),
                pl.BlockSpec((PAIRS_STEP, side), lambda s, k: (s, 0)),
                pl.BlockSpec((PAIRS_STEP, side, width), lambda s, k: (s, 0, 0)),
                pl.BlockSpec((half, side, width), lambda s, k: (0, 0, 0)),
            ],
            out_specs=pl.BlockSpec((half, side, width), lambda s, k: (0, 0, 0)),
        ),
        out_shape=jax.ShapeDtypeStruct((half, side, width), jnp.float32),
        compiler_params=pltpu.CompilerParams(dimension_semantics=("arbitrary",)),
        cost_estimate=pl.CostEstimate(
            flops=2 * pairs * side * side * width + 8 * pairs * side * side,
            transcendentals=pairs * side * side,
            bytes_accessed=pairs * side * (4 * side + 2 * width) + half * side * width * 6,
        ),
    )(keys, grids_t, source_duals, target_duals, rows, half_targets)


def squares(blocks_in):
    return jnp.sum(jnp.square(blocks_in.astype(jnp.float32)), axis=-1)


def pair_costs(source_rows, target_rows):
    inner_dot = jnp.einsum(
        "gid,gjd->gij", source_rows, target_rows, preferred_element_type=jnp.float32
    )
    inner_dot_t = jnp.einsum(
        "gjd,gid->gji", target_rows, source_rows, preferred_element_type=jnp.float32
    )
    source_sq = squares(source_rows)
    target_sq = squares(target_rows)
    width = source_rows.shape[2]
    grid = (source_sq[:, :, None] + target_sq[:, None, :] - 2.0 * inner_dot) / width
    grid_t = (source_sq[:, None, :] + target_sq[:, :, None] - 2.0 * inner_dot_t) / width
    return grid, grid_t


def pair_lse(scores, axis):
    peaks = jnp.max(scores, axis=axis)
    masses = jnp.sum(jnp.exp(scores - jnp.expand_dims(peaks, axis)), axis=axis)
    return peaks + jnp.log(masses)


def combine_by(values, block_key, key_count):
    member = (block_key[:, None] == jnp.arange(key_count)[None, :])[:, :, None]
    maxima = jnp.max(jnp.where(member, values[:, None, :], NEG_BIG), axis=0)
    shifts = jnp.where(member, values[:, None, :] - maxima[None, :, :], NEG_BIG)
    totals = jnp.sum(jnp.where(member, jnp.exp(shifts), 0.0), axis=0)
    return maxima, totals


def swap_rep(value):
    return lax.ppermute(value, "rep", [(0, 1), (1, 0)])


def a2a(value):
    return lax.all_to_all(value, "pts", split_axis=0, concat_axis=0, tiled=True)


def on_device(src_points, tgt_points, pair_source, pair_target, pair_count):
    peer_count = lax.axis_size("pts")
    point_rows, feat_width = src_points.shape
    block_len = BLOCK
    blocks = point_rows // block_len
    half_blocks = blocks // lax.axis_size("rep")
    rep_index = lax.axis_index("rep")
    lower_block = rep_index * half_blocks
    own_sources = src_points.reshape(blocks, block_len, feat_width)
    own_targets = tgt_points.reshape(blocks, block_len, feat_width)

    pair_total = pair_count[0]
    slot_total = pair_source.shape[0]
    usable = jnp.arange(slot_total) < pair_total
    source_local = jnp.where(usable, pair_source % blocks, 0)
    owner_ids = jnp.where(usable, pair_target // blocks, 0)
    target_local = jnp.where(usable, pair_target % blocks, 0)
    matched = (owner_ids[:, None] == jnp.arange(peer_count)[None, :]) & usable[:, None]
    wanted = jnp.max(jnp.where(matched, target_local[:, None], -1), axis=0)
    source_of_owner = jnp.max(jnp.where(matched, source_local[:, None], -1), axis=0)
    served = source_of_owner >= 0
    source_index = jnp.maximum(source_of_owner, 0)
    outgoing = own_sources[source_index]
    asked_ids = a2a(wanted)
    received = a2a(outgoing)

    valid = asked_ids >= 0
    half_key = jnp.where(valid, asked_ids - lower_block, -1)
    half_pick = jnp.clip(half_key, 0, half_blocks - 1)
    own_half = lax.dynamic_slice_in_dim(own_targets, lower_block, half_blocks, 0)
    pair_targets = own_half[half_pick]
    cost_grid, cost_grid_t = pair_costs(received, pair_targets)

    target_half = jnp.zeros((half_blocks, block_len), jnp.float32)
    for round_no in range(ITERS):
        target_here = target_half[half_pick]
        row_lse = sweep(cost_grid_t, target_here)
        row_back = a2a(row_lse)
        maxima, totals = combine_by(row_back, source_of_owner, blocks)
        other_maxima, other_totals = swap_rep((maxima, totals))
        merged = jnp.maximum(maxima, other_maxima)
        merged_totals = totals * jnp.exp(maxima - merged) + other_totals * jnp.exp(
            other_maxima - merged
        )
        source_dual = -EPSILON * (merged + jnp.log(merged_totals))
        sent_duals = jnp.where(served[:, None], source_dual[source_index], 0.0)
        source_here = a2a(sent_duals)
        column_lse = sweep(cost_grid, source_here)
        col_max, col_tot = combine_by(column_lse, half_key, half_blocks)
        target_half = -EPSILON * (col_max + jnp.log(col_tot))

    target_here = target_half[half_pick]
    gradient_half = gradient_sums(
        half_key, cost_grid_t, source_here, target_here, received, own_half
    )
    target_dual = lax.all_gather(target_half, "rep", axis=0, tiled=True)
    gradient = lax.all_gather(gradient_half, "rep", axis=0, tiled=True)
    return (
        source_dual.reshape(-1),
        target_dual.reshape(-1),
        gradient.reshape(blocks * block_len, feat_width),
    )


def solution(mesh):
    return jax.shard_map(
        on_device,
        mesh=mesh,
        in_specs=(
            P("pts", None),
            P("pts", None),
            P(("pts", "rep")),
            P(("pts", "rep")),
            P(("pts", "rep")),
        ),
        out_specs=(P("pts"), P("pts"), P("pts", None)),
        check_vma=False,
    )
```

```python
import functools

import jax
import jax.numpy as jnp
from jax import lax
from jax.experimental import pallas as pl
from jax.experimental.pallas import tpu as pltpu
from jax.sharding import PartitionSpec as P

BLOCK = 128
ITERS = 3


EPSILON = 0.05
NEG_BIG = -1e30
INV_EPS = 1.0 / EPSILON
PAIRS_STEP = 16


def as_column(row):
    side = row.shape[1]
    return jnp.transpose(jnp.broadcast_to(row, (side, side)))


def sweep_kernel(grid_ref, dual_ref, out_ref):
    def one(p, carry):
        dual_col = as_column(dual_ref[pl.ds(p, 1), :])
        scores = (dual_col - grid_ref[p]) * INV_EPS
        peak = jnp.max(scores, axis=0, keepdims=True)
        mass = jnp.sum(jnp.exp(scores - peak), axis=0, keepdims=True)
        out_ref[pl.ds(p, 1), :] = peak + jnp.log(mass)
        return carry

    lax.fori_loop(0, grid_ref.shape[0], one, 0)


def sweep(grids, duals):
    pairs, side, _ = grids.shape
    return pl.pallas_call(
        sweep_kernel,
        grid=(pairs // PAIRS_STEP,),
        in_specs=[
            pl.BlockSpec((PAIRS_STEP, side, side), lambda s: (s, 0, 0)),
            pl.BlockSpec((PAIRS_STEP, side), lambda s: (s, 0)),
        ],
        out_specs=pl.BlockSpec((PAIRS_STEP, side), lambda s: (s, 0)),
        out_shape=jax.ShapeDtypeStruct((pairs, side), jnp.float32),
        cost_estimate=pl.CostEstimate(
            flops=8 * pairs * side * side,
            transcendentals=pairs * side * side,
            bytes_accessed=4 * pairs * side * (side + 2),
        ),
    )(grids, duals)


def gradient_kernel(keys_ref, grid_t_ref, source_ref, target_ref, rows_ref, half_ref, out_ref):
    step = pl.program_id(0)

    @pl.when(step == 0)
    def _():
        out_ref[...] = jnp.zeros_like(out_ref)

    def one(p, carry):
        key = keys_ref[step * PAIRS_STEP + p]

        @pl.when(key >= 0)
        def _():
            target_col = as_column(target_ref[pl.ds(p, 1), :])
            plan_t = jnp.exp((source_ref[pl.ds(p, 1), :] + target_col - grid_t_ref[p]) * INV_EPS)
            mass = jnp.sum(plan_t, axis=1, keepdims=True)
            numerator = jnp.dot(
                plan_t.astype(jnp.bfloat16), rows_ref[p], preferred_element_type=jnp.float32
            )
            out_ref[key] += half_ref[key].astype(jnp.float32) * mass - numerator

        return carry

    lax.fori_loop(0, PAIRS_STEP, one, 0)


def gradient_sums(keys, grids_t, source_duals, target_duals, rows, half_targets):
    pairs, side, _ = grids_t.shape
    width = rows.shape[2]
    half = half_targets.shape[0]
    return pl.pallas_call(
        gradient_kernel,
        grid_spec=pltpu.PrefetchScalarGridSpec(
            num_scalar_prefetch=1,
            grid=(pairs // PAIRS_STEP,),
            in_specs=[
                pl.BlockSpec((PAIRS_STEP, side, side), lambda s, k: (s, 0, 0)),
                pl.BlockSpec((PAIRS_STEP, side), lambda s, k: (s, 0)),
                pl.BlockSpec((PAIRS_STEP, side), lambda s, k: (s, 0)),
                pl.BlockSpec((PAIRS_STEP, side, width), lambda s, k: (s, 0, 0)),
                pl.BlockSpec((half, side, width), lambda s, k: (0, 0, 0)),
            ],
            out_specs=pl.BlockSpec((half, side, width), lambda s, k: (0, 0, 0)),
        ),
        out_shape=jax.ShapeDtypeStruct((half, side, width), jnp.float32),
        compiler_params=pltpu.CompilerParams(dimension_semantics=("arbitrary",)),
        cost_estimate=pl.CostEstimate(
            flops=2 * pairs * side * side * width + 8 * pairs * side * side,
            transcendentals=pairs * side * side,
            bytes_accessed=pairs * side * (4 * side + 2 * width) + half * side * width * 6,
        ),
    )(keys, grids_t, source_duals, target_duals, rows, half_targets)


def squares(blocks_in):
    return jnp.sum(jnp.square(blocks_in.astype(jnp.float32)), axis=-1)


def pair_costs(source_rows, target_rows):
    inner_dot = jnp.einsum(
        "gid,gjd->gij", source_rows, target_rows, preferred_element_type=jnp.float32
    )
    inner_dot_t = jnp.einsum(
        "gjd,gid->gji", target_rows, source_rows, preferred_element_type=jnp.float32
    )
    source_sq = squares(source_rows)
    target_sq = squares(target_rows)
    width = source_rows.shape[2]
    grid = (source_sq[:, :, None] + target_sq[:, None, :] - 2.0 * inner_dot) / width
    grid_t = (source_sq[:, None, :] + target_sq[:, :, None] - 2.0 * inner_dot_t) / width
    return grid, grid_t


def pair_lse(scores, axis):
    peaks = jnp.max(scores, axis=axis)
    masses = jnp.sum(jnp.exp(scores - jnp.expand_dims(peaks, axis)), axis=axis)
    return peaks + jnp.log(masses)


def combine_by(values, block_key, key_count):
    member = (block_key[:, None] == jnp.arange(key_count)[None, :])[:, :, None]
    maxima = jnp.max(jnp.where(member, values[:, None, :], NEG_BIG), axis=0)
    shifts = jnp.where(member, values[:, None, :] - maxima[None, :, :], NEG_BIG)
    totals = jnp.sum(jnp.where(member, jnp.exp(shifts), 0.0), axis=0)
    return maxima, totals


def swap_rep(value):
    return lax.ppermute(value, "rep", [(0, 1), (1, 0)])


def a2a(value):
    return lax.all_to_all(value, "pts", split_axis=0, concat_axis=0, tiled=True)


def on_device(src_points, tgt_points, pair_source, pair_target, pair_count):
    peer_count = lax.axis_size("pts")
    point_rows, feat_width = src_points.shape
    block_len = BLOCK
    blocks = point_rows // block_len
    half_blocks = blocks // lax.axis_size("rep")
    rep_index = lax.axis_index("rep")
    lower_block = rep_index * half_blocks
    own_sources = src_points.reshape(blocks, block_len, feat_width)
    own_targets = tgt_points.reshape(blocks, block_len, feat_width)

    pair_total = pair_count[0]
    slot_total = pair_source.shape[0]
    usable = jnp.arange(slot_total) < pair_total
    source_local = jnp.where(usable, pair_source % blocks, 0)
    owner_ids = jnp.where(usable, pair_target // blocks, 0)
    target_local = jnp.where(usable, pair_target % blocks, 0)
    matched = (owner_ids[:, None] == jnp.arange(peer_count)[None, :]) & usable[:, None]
    wanted = jnp.max(jnp.where(matched, target_local[:, None], -1), axis=0)
    source_of_owner = jnp.max(jnp.where(matched, source_local[:, None], -1), axis=0)
    served = source_of_owner >= 0
    source_index = jnp.maximum(source_of_owner, 0)
    outgoing = own_sources[source_index]
    asked_ids = a2a(wanted)
    received = a2a(outgoing)

    valid = asked_ids >= 0
    half_key = jnp.where(valid, asked_ids - lower_block, -1)
    half_pick = jnp.clip(half_key, 0, half_blocks - 1)
    own_half = lax.dynamic_slice_in_dim(own_targets, lower_block, half_blocks, 0)
    pair_targets = own_half[half_pick]
    cost_grid, cost_grid_t = pair_costs(received, pair_targets)

    target_half = jnp.zeros((half_blocks, block_len), jnp.float32)
    for round_no in range(ITERS):
        target_here = target_half[half_pick]
        row_lse = pair_lse((target_here[:, None, :] - cost_grid) / EPSILON, 2)
        row_back = a2a(row_lse)
        maxima, totals = combine_by(row_back, source_of_owner, blocks)
        other_maxima, other_totals = swap_rep((maxima, totals))
        merged = jnp.maximum(maxima, other_maxima)
        merged_totals = totals * jnp.exp(maxima - merged) + other_totals * jnp.exp(
            other_maxima - merged
        )
        source_dual = -EPSILON * (merged + jnp.log(merged_totals))
        sent_duals = jnp.where(served[:, None], source_dual[source_index], 0.0)
        source_here = a2a(sent_duals)
        column_lse = pair_lse((source_here[:, :, None] - cost_grid) / EPSILON, 1)
        col_max, col_tot = combine_by(column_lse, half_key, half_blocks)
        target_half = -EPSILON * (col_max + jnp.log(col_tot))

    target_here = target_half[half_pick]
    gradient_half = gradient_sums(
        half_key, cost_grid_t, source_here, target_here, received, own_half
    )
    target_dual = lax.all_gather(target_half, "rep", axis=0, tiled=True)
    gradient = lax.all_gather(gradient_half, "rep", axis=0, tiled=True)
    return (
        source_dual.reshape(-1),
        target_dual.reshape(-1),
        gradient.reshape(blocks * block_len, feat_width),
    )


def solution(mesh):
    return jax.shard_map(
        on_device,
        mesh=mesh,
        in_specs=(
            P("pts", None),
            P("pts", None),
            P(("pts", "rep")),
            P(("pts", "rep")),
            P(("pts", "rep")),
        ),
        out_specs=(P("pts"), P("pts"), P("pts", None)),
        check_vma=False,
    )
```

```python
import jax
import jax.numpy as jnp
from jax import lax
from jax.experimental import pallas as pl
from jax.experimental.pallas import tpu as pltpu
from jax.sharding import PartitionSpec as P

BLOCK = 128
ITERS = 3


EPSILON = 0.05
NEG_BIG = -1e30
INV_EPS = 1.0 / EPSILON
SWEEP_STEP = 64
GRADIENT_STEP = 32


def columns_of(duals, step):
    pairs, side = duals.shape
    shaped = duals.reshape(pairs // step, step, side).transpose(0, 2, 1)
    return jnp.pad(shaped, ((0, 0), (0, 0), (0, side - step)))


def sweep_kernel(grid_ref, dual_ref, out_ref):
    side = grid_ref.shape[1]
    dual_cols = dual_ref[0]
    for p in range(grid_ref.shape[0]):
        dual_col = jnp.broadcast_to(dual_cols[:, p : p + 1], (side, side))
        scores = (dual_col - grid_ref[p]) * INV_EPS
        peak = jnp.max(scores, axis=0, keepdims=True)
        mass = jnp.sum(jnp.exp(scores - peak), axis=0, keepdims=True)
        out_ref[p : p + 1, :] = peak + jnp.log(mass)


def sweep(grids, duals):
    pairs, side, _ = grids.shape
    return pl.pallas_call(
        sweep_kernel,
        grid=(pairs // SWEEP_STEP,),
        in_specs=[
            pl.BlockSpec((SWEEP_STEP, side, side), lambda s: (s, 0, 0)),
            pl.BlockSpec((1, side, side), lambda s: (s, 0, 0)),
        ],
        out_specs=pl.BlockSpec((SWEEP_STEP, side), lambda s: (s, 0)),
        out_shape=jax.ShapeDtypeStruct((pairs, side), jnp.float32),
        cost_estimate=pl.CostEstimate(
            flops=8 * pairs * side * side,
            transcendentals=pairs * side * side,
            bytes_accessed=4 * pairs * side * (side + 2),
        ),
    )(grids, columns_of(duals, SWEEP_STEP))


def gradient_kernel(keys_ref, grid_t_ref, source_ref, target_ref, rows_ref, half_ref, out_ref):
    step = pl.program_id(0)
    side = grid_t_ref.shape[1]

    @pl.when(step == 0)
    def _():
        out_ref[...] = jnp.zeros_like(out_ref)

    target_cols = target_ref[0]
    for p in range(grid_t_ref.shape[0]):
        key = keys_ref[step * GRADIENT_STEP + p]

        @pl.when(key >= 0)
        def _():
            target_col = jnp.broadcast_to(target_cols[:, p : p + 1], (side, side))
            plan_t = jnp.exp((source_ref[p : p + 1, :] + target_col - grid_t_ref[p]) * INV_EPS)
            mass = jnp.sum(plan_t, axis=1, keepdims=True)
            numerator = jnp.dot(
                plan_t.astype(jnp.bfloat16), rows_ref[p], preferred_element_type=jnp.float32
            )
            out_ref[key] += half_ref[key].astype(jnp.float32) * mass - numerator


def gradient_sums(keys, grids_t, source_duals, target_duals, rows, half_targets):
    pairs, side, _ = grids_t.shape
    width = rows.shape[2]
    half = half_targets.shape[0]
    return pl.pallas_call(
        gradient_kernel,
        grid_spec=pltpu.PrefetchScalarGridSpec(
            num_scalar_prefetch=1,
            grid=(pairs // GRADIENT_STEP,),
            in_specs=[
                pl.BlockSpec((GRADIENT_STEP, side, side), lambda s, k: (s, 0, 0)),
                pl.BlockSpec((GRADIENT_STEP, side), lambda s, k: (s, 0)),
                pl.BlockSpec((1, side, side), lambda s, k: (s, 0, 0)),
                pl.BlockSpec((GRADIENT_STEP, side, width), lambda s, k: (s, 0, 0)),
                pl.BlockSpec((half, side, width), lambda s, k: (0, 0, 0)),
            ],
            out_specs=pl.BlockSpec((half, side, width), lambda s, k: (0, 0, 0)),
        ),
        out_shape=jax.ShapeDtypeStruct((half, side, width), jnp.float32),
        compiler_params=pltpu.CompilerParams(dimension_semantics=("arbitrary",)),
        cost_estimate=pl.CostEstimate(
            flops=2 * pairs * side * side * width + 8 * pairs * side * side,
            transcendentals=pairs * side * side,
            bytes_accessed=pairs * side * (4 * side + 2 * width) + half * side * width * 6,
        ),
    )(keys, grids_t, source_duals, columns_of(target_duals, GRADIENT_STEP), rows, half_targets)


def both_halves(mine, rep_index):
    other = lax.ppermute(mine, "rep", [(0, 1), (1, 0)])
    return jnp.where(
        rep_index == 0,
        jnp.concatenate([mine, other], axis=0),
        jnp.concatenate([other, mine], axis=0),
    )


def squares(blocks_in):
    return jnp.sum(jnp.square(blocks_in.astype(jnp.float32)), axis=-1)


def pair_costs(source_rows, target_rows):
    inner_dot = jnp.einsum(
        "gid,gjd->gij", source_rows, target_rows, preferred_element_type=jnp.float32
    )
    inner_dot_t = jnp.einsum(
        "gjd,gid->gji", target_rows, source_rows, preferred_element_type=jnp.float32
    )
    source_sq = squares(source_rows)
    target_sq = squares(target_rows)
    width = source_rows.shape[2]
    grid = (source_sq[:, :, None] + target_sq[:, None, :] - 2.0 * inner_dot) / width
    grid_t = (source_sq[:, None, :] + target_sq[:, :, None] - 2.0 * inner_dot_t) / width
    return grid, grid_t


def pair_lse(scores, axis):
    peaks = jnp.max(scores, axis=axis)
    masses = jnp.sum(jnp.exp(scores - jnp.expand_dims(peaks, axis)), axis=axis)
    return peaks + jnp.log(masses)


def combine_by(values, block_key, key_count):
    member = (block_key[:, None] == jnp.arange(key_count)[None, :])[:, :, None]
    maxima = jnp.max(jnp.where(member, values[:, None, :], NEG_BIG), axis=0)
    shifts = jnp.where(member, values[:, None, :] - maxima[None, :, :], NEG_BIG)
    totals = jnp.sum(jnp.where(member, jnp.exp(shifts), 0.0), axis=0)
    return maxima, totals


def swap_rep(value):
    return lax.ppermute(value, "rep", [(0, 1), (1, 0)])


def a2a(value):
    return lax.all_to_all(value, "pts", split_axis=0, concat_axis=0, tiled=True)


def on_device(src_points, tgt_points, pair_source, pair_target, pair_count):
    peer_count = lax.axis_size("pts")
    point_rows, feat_width = src_points.shape
    block_len = BLOCK
    blocks = point_rows // block_len
    half_blocks = blocks // lax.axis_size("rep")
    rep_index = lax.axis_index("rep")
    lower_block = rep_index * half_blocks
    own_sources = src_points.reshape(blocks, block_len, feat_width)
    own_targets = tgt_points.reshape(blocks, block_len, feat_width)

    pair_total = pair_count[0]
    slot_total = pair_source.shape[0]
    usable = jnp.arange(slot_total) < pair_total
    source_local = jnp.where(usable, pair_source % blocks, 0)
    owner_ids = jnp.where(usable, pair_target // blocks, 0)
    target_local = jnp.where(usable, pair_target % blocks, 0)
    matched = (owner_ids[:, None] == jnp.arange(peer_count)[None, :]) & usable[:, None]
    wanted = jnp.max(jnp.where(matched, target_local[:, None], -1), axis=0)
    source_of_owner = jnp.max(jnp.where(matched, source_local[:, None], -1), axis=0)
    served = source_of_owner >= 0
    source_index = jnp.maximum(source_of_owner, 0)
    outgoing = own_sources[source_index]
    asked_ids = a2a(wanted)
    received = a2a(outgoing)

    valid = asked_ids >= 0
    half_key = jnp.where(valid, asked_ids - lower_block, -1)
    half_pick = jnp.clip(half_key, 0, half_blocks - 1)
    own_half = lax.dynamic_slice_in_dim(own_targets, lower_block, half_blocks, 0)
    pair_targets = own_half[half_pick]
    cost_grid, cost_grid_t = pair_costs(received, pair_targets)

    target_half = jnp.zeros((half_blocks, block_len), jnp.float32)
    for round_no in range(ITERS):
        target_here = target_half[half_pick]
        row_lse = sweep(cost_grid_t, target_here)
        row_back = a2a(row_lse)
        maxima, totals = combine_by(row_back, source_of_owner, blocks)
        other_maxima, other_totals = swap_rep((maxima, totals))
        merged = jnp.maximum(maxima, other_maxima)
        merged_totals = totals * jnp.exp(maxima - merged) + other_totals * jnp.exp(
            other_maxima - merged
        )
        source_dual = -EPSILON * (merged + jnp.log(merged_totals))
        sent_duals = jnp.where(served[:, None], source_dual[source_index], 0.0)
        source_here = a2a(sent_duals)
        column_lse = sweep(cost_grid, source_here)
        col_max, col_tot = combine_by(column_lse, half_key, half_blocks)
        target_half = -EPSILON * (col_max + jnp.log(col_tot))

    target_here = target_half[half_pick]
    gradient_half = gradient_sums(
        half_key, cost_grid_t, source_here, target_here, received, own_half
    )
    target_dual = both_halves(target_half, rep_index)
    gradient = both_halves(gradient_half, rep_index)
    return (
        source_dual.reshape(-1),
        target_dual.reshape(-1),
        gradient.reshape(blocks * block_len, feat_width),
    )


def solution(mesh):
    return jax.shard_map(
        on_device,
        mesh=mesh,
        in_specs=(
            P("pts", None),
            P("pts", None),
            P(("pts", "rep")),
            P(("pts", "rep")),
            P(("pts", "rep")),
        ),
        out_specs=(P("pts"), P("pts"), P("pts", None)),
        check_vma=False,
    )
```

```python
import jax
import jax.numpy as jnp
from jax import lax
from jax.experimental import pallas as pl
from jax.experimental.pallas import tpu as pltpu
from jax.sharding import PartitionSpec as P

BLOCK = 128
ITERS = 3


EPSILON = 0.05
NEG_BIG = -1e30
INV_EPS = 1.0 / EPSILON
SWEEP_STEP = 64
GRADIENT_STEP = 32


def columns_of(duals, step):
    pairs, side = duals.shape
    shaped = duals.reshape(pairs // step, step, side).transpose(0, 2, 1)
    return jnp.pad(shaped, ((0, 0), (0, 0), (0, side - step)))


def sweep_kernel(grid_ref, dual_ref, out_ref):
    side = grid_ref.shape[1]
    dual_cols = dual_ref[0]
    for p in range(grid_ref.shape[0]):
        dual_col = jnp.broadcast_to(dual_cols[:, p : p + 1], (side, side))
        scores = (dual_col - grid_ref[p]) * INV_EPS
        peak = jnp.max(scores, axis=0, keepdims=True)
        mass = jnp.sum(jnp.exp(scores - peak), axis=0, keepdims=True)
        out_ref[p : p + 1, :] = peak + jnp.log(mass)


def sweep(grids, duals):
    pairs, side, _ = grids.shape
    return pl.pallas_call(
        sweep_kernel,
        grid=(pairs // SWEEP_STEP,),
        in_specs=[
            pl.BlockSpec((SWEEP_STEP, side, side), lambda s: (s, 0, 0)),
            pl.BlockSpec((1, side, side), lambda s: (s, 0, 0)),
        ],
        out_specs=pl.BlockSpec((SWEEP_STEP, side), lambda s: (s, 0)),
        out_shape=jax.ShapeDtypeStruct((pairs, side), jnp.float32),
        cost_estimate=pl.CostEstimate(
            flops=8 * pairs * side * side,
            transcendentals=pairs * side * side,
            bytes_accessed=4 * pairs * side * (side + 2),
        ),
    )(grids, columns_of(duals, SWEEP_STEP))


def gradient_kernel(keys_ref, grid_t_ref, source_ref, target_ref, rows_ref, half_ref, out_ref):
    step = pl.program_id(0)
    side = grid_t_ref.shape[1]

    @pl.when(step == 0)
    def _():
        out_ref[...] = jnp.zeros_like(out_ref)

    target_cols = target_ref[0]
    for p in range(grid_t_ref.shape[0]):
        key = keys_ref[step * GRADIENT_STEP + p]

        @pl.when(key >= 0)
        def _():
            target_col = jnp.broadcast_to(target_cols[:, p : p + 1], (side, side))
            plan_t = jnp.exp((source_ref[p : p + 1, :] + target_col - grid_t_ref[p]) * INV_EPS)
            mass = jnp.sum(plan_t, axis=1, keepdims=True)
            numerator = jnp.dot(
                plan_t.astype(jnp.bfloat16), rows_ref[p], preferred_element_type=jnp.float32
            )
            out_ref[key] += half_ref[key].astype(jnp.float32) * mass - numerator


def gradient_sums(keys, grids_t, source_duals, target_duals, rows, half_targets):
    pairs, side, _ = grids_t.shape
    width = rows.shape[2]
    half = half_targets.shape[0]
    return pl.pallas_call(
        gradient_kernel,
        grid_spec=pltpu.PrefetchScalarGridSpec(
            num_scalar_prefetch=1,
            grid=(pairs // GRADIENT_STEP,),
            in_specs=[
                pl.BlockSpec((GRADIENT_STEP, side, side), lambda s, k: (s, 0, 0)),
                pl.BlockSpec((GRADIENT_STEP, side), lambda s, k: (s, 0)),
                pl.BlockSpec((1, side, side), lambda s, k: (s, 0, 0)),
                pl.BlockSpec((GRADIENT_STEP, side, width), lambda s, k: (s, 0, 0)),
                pl.BlockSpec((half, side, width), lambda s, k: (0, 0, 0)),
            ],
            out_specs=pl.BlockSpec((half, side, width), lambda s, k: (0, 0, 0)),
        ),
        out_shape=jax.ShapeDtypeStruct((half, side, width), jnp.float32),
        compiler_params=pltpu.CompilerParams(dimension_semantics=("arbitrary",)),
        cost_estimate=pl.CostEstimate(
            flops=2 * pairs * side * side * width + 8 * pairs * side * side,
            transcendentals=pairs * side * side,
            bytes_accessed=pairs * side * (4 * side + 2 * width) + half * side * width * 6,
        ),
    )(keys, grids_t, source_duals, columns_of(target_duals, GRADIENT_STEP), rows, half_targets)


def both_halves(mine, rep_index):
    other = lax.ppermute(mine, "rep", [(0, 1), (1, 0)])
    return jnp.where(
        rep_index == 0,
        jnp.concatenate([mine, other], axis=0),
        jnp.concatenate([other, mine], axis=0),
    )


def squares(blocks_in):
    return jnp.sum(jnp.square(blocks_in.astype(jnp.float32)), axis=-1)


def pair_costs(source_rows, target_rows):
    inner_dot = jnp.einsum(
        "gid,gjd->gij", source_rows, target_rows, preferred_element_type=jnp.float32
    )
    inner_dot_t = jnp.einsum(
        "gjd,gid->gji", target_rows, source_rows, preferred_element_type=jnp.float32
    )
    source_sq = squares(source_rows)
    target_sq = squares(target_rows)
    width = source_rows.shape[2]
    grid = (source_sq[:, :, None] + target_sq[:, None, :] - 2.0 * inner_dot) / width
    grid_t = (source_sq[:, None, :] + target_sq[:, :, None] - 2.0 * inner_dot_t) / width
    return grid, grid_t


def combine_by(values, block_key, key_count):
    member = (block_key[:, None] == jnp.arange(key_count)[None, :])[:, :, None]
    maxima = jnp.max(jnp.where(member, values[:, None, :], NEG_BIG), axis=0)
    shifts = jnp.where(member, values[:, None, :] - maxima[None, :, :], NEG_BIG)
    totals = jnp.sum(jnp.where(member, jnp.exp(shifts), 0.0), axis=0)
    return maxima, totals


def swap_rep(value):
    return lax.ppermute(value, "rep", [(0, 1), (1, 0)])


def a2a(value):
    return lax.all_to_all(value, "pts", split_axis=0, concat_axis=0, tiled=True)


def on_device(src_points, tgt_points, pair_source, pair_target, pair_count):
    peer_count = lax.axis_size("pts")
    point_rows, feat_width = src_points.shape
    block_len = BLOCK
    blocks = point_rows // block_len
    half_blocks = blocks // lax.axis_size("rep")
    rep_index = lax.axis_index("rep")
    lower_block = rep_index * half_blocks
    own_sources = src_points.reshape(blocks, block_len, feat_width)
    own_targets = tgt_points.reshape(blocks, block_len, feat_width)

    pair_total = pair_count[0]
    slot_total = pair_source.shape[0]
    usable = jnp.arange(slot_total) < pair_total
    source_local = jnp.where(usable, pair_source % blocks, 0)
    owner_ids = jnp.where(usable, pair_target // blocks, 0)
    target_local = jnp.where(usable, pair_target % blocks, 0)
    matched = (owner_ids[:, None] == jnp.arange(peer_count)[None, :]) & usable[:, None]
    wanted = jnp.max(jnp.where(matched, target_local[:, None], -1), axis=0)
    source_of_owner = jnp.max(jnp.where(matched, source_local[:, None], -1), axis=0)
    served = source_of_owner >= 0
    source_index = jnp.maximum(source_of_owner, 0)
    outgoing = own_sources[source_index]
    received = a2a(outgoing)
    every_wanted = lax.all_gather(wanted, "pts")
    asked_ids = lax.dynamic_index_in_dim(every_wanted, lax.axis_index("pts"), 1, False)

    valid = asked_ids >= 0
    half_key = jnp.where(valid, asked_ids - lower_block, -1)
    half_pick = jnp.clip(half_key, 0, half_blocks - 1)
    own_half = lax.dynamic_slice_in_dim(own_targets, lower_block, half_blocks, 0)
    pair_targets = own_half[half_pick]
    cost_grid, cost_grid_t = pair_costs(received, pair_targets)

    target_half = jnp.zeros((half_blocks, block_len), jnp.float32)
    for _ in range(ITERS):
        target_here = target_half[half_pick]
        row_lse = sweep(cost_grid_t, target_here)
        row_back = a2a(row_lse)
        maxima, totals = combine_by(row_back, source_of_owner, blocks)
        other_maxima, other_totals = swap_rep((maxima, totals))
        merged = jnp.maximum(maxima, other_maxima)
        merged_totals = totals * jnp.exp(maxima - merged) + other_totals * jnp.exp(
            other_maxima - merged
        )
        source_dual = -EPSILON * (merged + jnp.log(merged_totals))
        sent_duals = jnp.where(served[:, None], source_dual[source_index], 0.0)
        source_here = a2a(sent_duals)
        column_lse = sweep(cost_grid, source_here)
        col_max, col_tot = combine_by(column_lse, half_key, half_blocks)
        target_half = -EPSILON * (col_max + jnp.log(col_tot))

    target_here = target_half[half_pick]
    gradient_half = gradient_sums(
        half_key, cost_grid_t, source_here, target_here, received, own_half
    )
    target_dual = both_halves(target_half, rep_index)
    gradient = both_halves(gradient_half, rep_index)
    return (
        source_dual.reshape(-1),
        target_dual.reshape(-1),
        gradient.reshape(blocks * block_len, feat_width),
    )


def solution(mesh):
    return jax.shard_map(
        on_device,
        mesh=mesh,
        in_specs=(
            P("pts", None),
            P("pts", None),
            P(("pts", "rep")),
            P(("pts", "rep")),
            P(("pts", "rep")),
        ),
        out_specs=(P("pts"), P("pts"), P("pts", None)),
        check_vma=False,
    )
```

```python
import jax
import jax.numpy as jnp
from jax import lax
from jax.experimental import pallas as pl
from jax.experimental.pallas import tpu as pltpu
from jax.sharding import PartitionSpec as P

BLOCK = 128
ITERS = 3


EPSILON = 0.05
NEG_BIG = -1e30
INV_EPS = 1.0 / EPSILON
SWEEP_STEP = 64
GRADIENT_STEP = 32


def columns_of(duals, step):
    pairs, side = duals.shape
    shaped = duals.reshape(pairs // step, step, side).transpose(0, 2, 1)
    return jnp.pad(shaped, ((0, 0), (0, 0), (0, side - step)))


def sweep_kernel(grid_ref, dual_ref, out_ref):
    side = grid_ref.shape[1]
    dual_cols = dual_ref[0]
    for p in range(grid_ref.shape[0]):
        dual_col = jnp.broadcast_to(dual_cols[:, p : p + 1], (side, side))
        scores = (dual_col - grid_ref[p]) * INV_EPS
        peak = jnp.max(scores, axis=0, keepdims=True)
        mass = jnp.sum(jnp.exp(scores - peak), axis=0, keepdims=True)
        out_ref[p : p + 1, :] = peak + jnp.log(mass)


def sweep(grids, duals):
    pairs, side, _ = grids.shape
    return pl.pallas_call(
        sweep_kernel,
        grid=(pairs // SWEEP_STEP,),
        in_specs=[
            pl.BlockSpec((SWEEP_STEP, side, side), lambda s: (s, 0, 0)),
            pl.BlockSpec((1, side, side), lambda s: (s, 0, 0)),
        ],
        out_specs=pl.BlockSpec((SWEEP_STEP, side), lambda s: (s, 0)),
        out_shape=jax.ShapeDtypeStruct((pairs, side), jnp.float32),
        cost_estimate=pl.CostEstimate(
            flops=8 * pairs * side * side,
            transcendentals=pairs * side * side,
            bytes_accessed=4 * pairs * side * (side + 2),
        ),
    )(grids, columns_of(duals, SWEEP_STEP))


def gradient_kernel(
    keys_ref, grid_t_ref, source_ref, target_ref, rows_ref, half_ref, out_ref, mass_ref
):
    step = pl.program_id(0)
    side = grid_t_ref.shape[1]

    @pl.when(step == 0)
    def _():
        out_ref[...] = jnp.zeros_like(out_ref)
        mass_ref[...] = jnp.zeros_like(mass_ref)

    target_cols = target_ref[0]
    ones = jnp.ones((side, side), jnp.bfloat16)
    for p in range(grid_t_ref.shape[0]):
        key = keys_ref[step * GRADIENT_STEP + p]
        slot = jnp.maximum(key, 0)
        target_col = jnp.broadcast_to(target_cols[:, p : p + 1], (side, side))
        plan_t = jnp.exp((source_ref[p : p + 1, :] + target_col - grid_t_ref[p]) * INV_EPS)
        plan_t = jnp.where(key >= 0, plan_t, 0.0)
        weights = plan_t.astype(jnp.bfloat16)
        remainder = (plan_t - weights.astype(jnp.float32)).astype(jnp.bfloat16)
        mass = jnp.dot(weights, ones, preferred_element_type=jnp.float32) + jnp.dot(
            remainder, ones, preferred_element_type=jnp.float32
        )
        numerator = jnp.dot(weights, rows_ref[p], preferred_element_type=jnp.float32)
        out_ref[slot] -= numerator
        mass_ref[slot] += mass

    @pl.when(step == pl.num_programs(0) - 1)
    def _():
        mass = mass_ref[...]
        out_ref[...] += half_ref[...].astype(jnp.float32) * jnp.concatenate([mass, mass], axis=2)


def gradient_sums(keys, grids_t, source_duals, target_duals, rows, half_targets):
    pairs, side, _ = grids_t.shape
    width = rows.shape[2]
    half = half_targets.shape[0]
    return pl.pallas_call(
        gradient_kernel,
        grid_spec=pltpu.PrefetchScalarGridSpec(
            num_scalar_prefetch=1,
            grid=(pairs // GRADIENT_STEP,),
            in_specs=[
                pl.BlockSpec((GRADIENT_STEP, side, side), lambda s, k: (s, 0, 0)),
                pl.BlockSpec((GRADIENT_STEP, side), lambda s, k: (s, 0)),
                pl.BlockSpec((1, side, side), lambda s, k: (s, 0, 0)),
                pl.BlockSpec((GRADIENT_STEP, side, width), lambda s, k: (s, 0, 0)),
                pl.BlockSpec((half, side, width), lambda s, k: (0, 0, 0)),
            ],
            out_specs=pl.BlockSpec((half, side, width), lambda s, k: (0, 0, 0)),
            scratch_shapes=[pltpu.VMEM((half, side, side), jnp.float32)],
        ),
        out_shape=jax.ShapeDtypeStruct((half, side, width), jnp.float32),
        compiler_params=pltpu.CompilerParams(dimension_semantics=("arbitrary",)),
        cost_estimate=pl.CostEstimate(
            flops=2 * pairs * side * side * width + 8 * pairs * side * side,
            transcendentals=pairs * side * side,
            bytes_accessed=pairs * side * (4 * side + 2 * width) + half * side * width * 6,
        ),
    )(keys, grids_t, source_duals, columns_of(target_duals, GRADIENT_STEP), rows, half_targets)


def both_halves(mine, rep_index):
    other = lax.ppermute(mine, "rep", [(0, 1), (1, 0)])
    return jnp.where(
        rep_index == 0,
        jnp.concatenate([mine, other], axis=0),
        jnp.concatenate([other, mine], axis=0),
    )


def squares(blocks_in):
    return jnp.sum(jnp.square(blocks_in.astype(jnp.float32)), axis=-1)


def pair_costs(source_rows, target_rows, source_sq, target_sq):
    inner_dot = jnp.einsum(
        "gid,gjd->gij", source_rows, target_rows, preferred_element_type=jnp.float32
    )
    inner_dot_t = jnp.einsum(
        "gjd,gid->gji", target_rows, source_rows, preferred_element_type=jnp.float32
    )
    width = source_rows.shape[2]
    grid = (source_sq[:, :, None] + target_sq[:, None, :] - 2.0 * inner_dot) / width
    grid_t = (source_sq[:, None, :] + target_sq[:, :, None] - 2.0 * inner_dot_t) / width
    return grid, grid_t


def pair_lse(scores, axis):
    peaks = jnp.max(scores, axis=axis)
    masses = jnp.sum(jnp.exp(scores - jnp.expand_dims(peaks, axis)), axis=axis)
    return peaks + jnp.log(masses)


def combine_by(values, block_key, key_count):
    member = (block_key[:, None] == jnp.arange(key_count)[None, :])[:, :, None]
    maxima = jnp.max(jnp.where(member, values[:, None, :], NEG_BIG), axis=0)
    shifts = jnp.where(member, values[:, None, :] - maxima[None, :, :], NEG_BIG)
    totals = jnp.sum(jnp.where(member, jnp.exp(shifts), 0.0), axis=0)
    return maxima, totals


def swap_rep(value):
    return lax.ppermute(value, "rep", [(0, 1), (1, 0)])


def a2a(value):
    return lax.all_to_all(value, "pts", split_axis=0, concat_axis=0, tiled=True)


def on_device(src_points, tgt_points, pair_source, pair_target, pair_count):
    peer_count = lax.axis_size("pts")
    point_rows, feat_width = src_points.shape
    block_len = BLOCK
    blocks = point_rows // block_len
    half_blocks = blocks // lax.axis_size("rep")
    rep_index = lax.axis_index("rep")
    lower_block = rep_index * half_blocks
    own_sources = src_points.reshape(blocks, block_len, feat_width)
    own_targets = tgt_points.reshape(blocks, block_len, feat_width)

    pair_total = pair_count[0]
    slot_total = pair_source.shape[0]
    usable = jnp.arange(slot_total) < pair_total
    source_local = jnp.where(usable, pair_source % blocks, 0)
    owner_ids = jnp.where(usable, pair_target // blocks, 0)
    target_local = jnp.where(usable, pair_target % blocks, 0)
    matched = (owner_ids[:, None] == jnp.arange(peer_count)[None, :]) & usable[:, None]
    wanted = jnp.max(jnp.where(matched, target_local[:, None], -1), axis=0)
    source_of_owner = jnp.max(jnp.where(matched, source_local[:, None], -1), axis=0)
    served = source_of_owner >= 0
    source_index = jnp.maximum(source_of_owner, 0)
    outgoing = own_sources[source_index]
    asked_info = jnp.stack(
        [
            squares(own_sources)[source_index],
            jnp.broadcast_to(wanted.astype(jnp.float32)[:, None], (peer_count, block_len)),
        ],
        axis=1,
    )
    asked_info = a2a(asked_info)
    received = a2a(outgoing)
    asked_ids = asked_info[:, 1, 0].astype(jnp.int32)
    received_sq = asked_info[:, 0, :]

    valid = asked_ids >= 0
    half_key = jnp.where(valid, asked_ids - lower_block, -1)
    half_pick = jnp.clip(half_key, 0, half_blocks - 1)
    own_half = lax.dynamic_slice_in_dim(own_targets, lower_block, half_blocks, 0)
    pair_targets = own_half[half_pick]
    target_sq = squares(own_half)[half_pick]
    cost_grid, cost_grid_t = pair_costs(received, pair_targets, received_sq, target_sq)

    target_half = jnp.zeros((half_blocks, block_len), jnp.float32)
    for round_no in range(ITERS):
        target_here = target_half[half_pick]
        row_lse = sweep(cost_grid_t, target_here)
        row_back = a2a(row_lse)
        maxima, totals = combine_by(row_back, source_of_owner, blocks)
        other_maxima, other_totals = swap_rep((maxima, totals))
        merged = jnp.maximum(maxima, other_maxima)
        merged_totals = totals * jnp.exp(maxima - merged) + other_totals * jnp.exp(
            other_maxima - merged
        )
        source_dual = -EPSILON * (merged + jnp.log(merged_totals))
        sent_duals = jnp.where(served[:, None], source_dual[source_index], 0.0)
        source_here = a2a(sent_duals)
        column_lse = sweep(cost_grid, source_here)
        col_max, col_tot = combine_by(column_lse, half_key, half_blocks)
        target_half = -EPSILON * (col_max + jnp.log(col_tot))

    target_here = target_half[half_pick]
    gradient_half = gradient_sums(
        half_key, cost_grid_t, source_here, target_here, received, own_half
    )
    target_dual = both_halves(target_half, rep_index)
    gradient = both_halves(gradient_half, rep_index)
    return (
        source_dual.reshape(-1),
        target_dual.reshape(-1),
        gradient.reshape(blocks * block_len, feat_width),
    )


def solution(mesh):
    return jax.shard_map(
        on_device,
        mesh=mesh,
        in_specs=(
            P("pts", None),
            P("pts", None),
            P(("pts", "rep")),
            P(("pts", "rep")),
            P(("pts", "rep")),
        ),
        out_specs=(P("pts"), P("pts"), P("pts", None)),
        check_vma=False,
    )
```

```python
import jax
import jax.numpy as jnp
from jax import lax
from jax.experimental import pallas as pl
from jax.experimental.pallas import tpu as pltpu
from jax.sharding import PartitionSpec as P

BLOCK = 128
ITERS = 3


EPSILON = 0.05
NEG_BIG = -1e30
INV_EPS = 1.0 / EPSILON
SWEEP_STEP = 64
GRADIENT_STEP = 32


def columns_of(duals, step):
    pairs, side = duals.shape
    shaped = duals.reshape(pairs // step, step, side).transpose(0, 2, 1)
    return jnp.pad(shaped, ((0, 0), (0, 0), (0, side - step)))


def sweep_kernel(grid_ref, dual_ref, out_ref):
    side = grid_ref.shape[1]
    dual_cols = dual_ref[0]
    for p in range(grid_ref.shape[0]):
        dual_col = jnp.broadcast_to(dual_cols[:, p : p + 1], (side, side))
        scores = dual_col - grid_ref[p]
        peak = jnp.max(scores, axis=0, keepdims=True)
        mass = jnp.sum(jnp.exp(scores - peak), axis=0, keepdims=True)
        out_ref[p : p + 1, :] = peak + jnp.log(mass)


def sweep(grids, duals):
    pairs, side, _ = grids.shape
    return pl.pallas_call(
        sweep_kernel,
        grid=(pairs // SWEEP_STEP,),
        in_specs=[
            pl.BlockSpec((SWEEP_STEP, side, side), lambda s: (s, 0, 0)),
            pl.BlockSpec((1, side, side), lambda s: (s, 0, 0)),
        ],
        out_specs=pl.BlockSpec((SWEEP_STEP, side), lambda s: (s, 0)),
        out_shape=jax.ShapeDtypeStruct((pairs, side), jnp.float32),
        cost_estimate=pl.CostEstimate(
            flops=8 * pairs * side * side,
            transcendentals=pairs * side * side,
            bytes_accessed=4 * pairs * side * (side + 2),
        ),
    )(grids, columns_of(duals, SWEEP_STEP))


def gradient_kernel(
    keys_ref, place_ref, grid_t_ref, source_ref, target_ref, rows_ref, half_ref, out_ref, mass_ref
):
    step = pl.program_id(0)
    side = grid_t_ref.shape[1]

    @pl.when(step == 0)
    def _():
        out_ref[...] = jnp.zeros_like(out_ref)
        mass_ref[...] = jnp.zeros_like(mass_ref)

    target_cols = target_ref[0]
    ones = jnp.ones((side, side), jnp.bfloat16)
    for p in range(grid_t_ref.shape[0]):
        key = keys_ref[step * GRADIENT_STEP + p]
        slot = jnp.maximum(key, 0)
        target_col = jnp.broadcast_to(target_cols[:, p : p + 1], (side, side))
        plan_t = jnp.exp(source_ref[p : p + 1, :] + target_col - grid_t_ref[p])
        plan_t = jnp.where(key >= 0, plan_t, 0.0)
        weights = plan_t.astype(jnp.bfloat16)
        remainder = (plan_t - weights.astype(jnp.float32)).astype(jnp.bfloat16)
        mass = jnp.dot(weights, ones, preferred_element_type=jnp.float32) + jnp.dot(
            remainder, ones, preferred_element_type=jnp.float32
        )
        numerator = jnp.dot(weights, rows_ref[p], preferred_element_type=jnp.float32)
        out_ref[slot] -= numerator
        mass_ref[slot] += mass

    @pl.when(step == pl.num_programs(0) - 1)
    def _():
        mass = mass_ref[...]
        out_ref[...] += half_ref[...].astype(jnp.float32) * jnp.concatenate([mass, mass], axis=2)


def gradient_sums(keys, place, grids_t, source_duals, target_duals, rows, half_targets):
    pairs, side, _ = grids_t.shape
    width = rows.shape[2]
    half = half_targets.shape[0]
    return pl.pallas_call(
        gradient_kernel,
        grid_spec=pltpu.PrefetchScalarGridSpec(
            num_scalar_prefetch=2,
            grid=(pairs // GRADIENT_STEP,),
            in_specs=[
                pl.BlockSpec((GRADIENT_STEP, side, side), lambda s, k, w: (s, 0, 0)),
                pl.BlockSpec((GRADIENT_STEP, side), lambda s, k, w: (s, 0)),
                pl.BlockSpec((1, side, side), lambda s, k, w: (s, 0, 0)),
                pl.BlockSpec((GRADIENT_STEP, side, width), lambda s, k, w: (s, 0, 0)),
                pl.BlockSpec((half, side, width), lambda s, k, w: (0, 0, 0)),
            ],
            out_specs=pl.BlockSpec((half, side, width), lambda s, k, w: (w[0], 0, 0)),
            scratch_shapes=[pltpu.VMEM((half, side, side), jnp.float32)],
        ),
        out_shape=jax.ShapeDtypeStruct((2 * half, side, width), jnp.float32),
        compiler_params=pltpu.CompilerParams(dimension_semantics=("arbitrary",)),
        cost_estimate=pl.CostEstimate(
            flops=2 * pairs * side * side * width + 8 * pairs * side * side,
            transcendentals=pairs * side * side,
            bytes_accessed=pairs * side * (4 * side + 2 * width) + half * side * width * 6,
        ),
    )(keys, place, grids_t, source_duals, columns_of(target_duals, GRADIENT_STEP), rows, half_targets)


def both_halves(mine, rep_index):
    other = lax.ppermute(mine, "rep", [(0, 1), (1, 0)])
    return jnp.where(
        rep_index == 0,
        jnp.concatenate([mine, other], axis=0),
        jnp.concatenate([other, mine], axis=0),
    )


def squares(blocks_in):
    return jnp.sum(jnp.square(blocks_in.astype(jnp.float32)), axis=-1)


def pair_costs(source_rows, target_rows, source_sq, target_sq):
    inner_dot = jnp.einsum(
        "gid,gjd->gij", source_rows, target_rows, preferred_element_type=jnp.float32
    )
    inner_dot_t = jnp.einsum(
        "gjd,gid->gji", target_rows, source_rows, preferred_element_type=jnp.float32
    )
    scale = INV_EPS / source_rows.shape[2]
    grid = (source_sq[:, :, None] + target_sq[:, None, :] - 2.0 * inner_dot) * scale
    grid_t = (source_sq[:, None, :] + target_sq[:, :, None] - 2.0 * inner_dot_t) * scale
    return grid, grid_t


def pair_lse(scores, axis):
    peaks = jnp.max(scores, axis=axis)
    masses = jnp.sum(jnp.exp(scores - jnp.expand_dims(peaks, axis)), axis=axis)
    return peaks + jnp.log(masses)


def combine_by(values, block_key, key_count):
    member = (block_key[:, None] == jnp.arange(key_count)[None, :])[:, :, None]
    maxima = jnp.max(jnp.where(member, values[:, None, :], NEG_BIG), axis=0)
    shifts = jnp.where(member, values[:, None, :] - maxima[None, :, :], NEG_BIG)
    totals = jnp.sum(jnp.where(member, jnp.exp(shifts), 0.0), axis=0)
    return maxima, totals


def swap_rep(value):
    return lax.ppermute(value, "rep", [(0, 1), (1, 0)])


def a2a(value):
    return lax.all_to_all(value, "pts", split_axis=0, concat_axis=0, tiled=True)


def on_device(src_points, tgt_points, pair_source, pair_target, pair_count):
    peer_count = lax.axis_size("pts")
    point_rows, feat_width = src_points.shape
    block_len = BLOCK
    blocks = point_rows // block_len
    half_blocks = blocks // lax.axis_size("rep")
    rep_index = lax.axis_index("rep")
    lower_block = rep_index * half_blocks
    own_sources = src_points.reshape(blocks, block_len, feat_width)
    own_targets = tgt_points.reshape(blocks, block_len, feat_width)

    pair_total = pair_count[0]
    slot_total = pair_source.shape[0]
    usable = jnp.arange(slot_total) < pair_total
    source_local = jnp.where(usable, pair_source % blocks, 0)
    owner_ids = jnp.where(usable, pair_target // blocks, 0)
    target_local = jnp.where(usable, pair_target % blocks, 0)
    matched = (owner_ids[:, None] == jnp.arange(peer_count)[None, :]) & usable[:, None]
    wanted = jnp.max(jnp.where(matched, target_local[:, None], -1), axis=0)
    source_of_owner = jnp.max(jnp.where(matched, source_local[:, None], -1), axis=0)
    served = source_of_owner >= 0
    source_index = jnp.maximum(source_of_owner, 0)
    outgoing = own_sources[source_index]
    asked_info = jnp.stack(
        [
            squares(own_sources)[source_index],
            jnp.broadcast_to(wanted.astype(jnp.float32)[:, None], (peer_count, block_len)),
        ],
        axis=1,
    )
    asked_info = a2a(asked_info)
    received = a2a(outgoing)
    asked_ids = asked_info[:, 1, 0].astype(jnp.int32)
    received_sq = asked_info[:, 0, :]

    valid = asked_ids >= 0
    half_key = jnp.where(valid, asked_ids - lower_block, -1)
    half_pick = jnp.clip(half_key, 0, half_blocks - 1)
    own_half = lax.dynamic_slice_in_dim(own_targets, lower_block, half_blocks, 0)
    pair_targets = own_half[half_pick]
    target_sq = squares(own_half)[half_pick]
    cost_grid, cost_grid_t = pair_costs(received, pair_targets, received_sq, target_sq)

    target_half = jnp.zeros((half_blocks, block_len), jnp.float32)
    for round_no in range(ITERS):
        target_here = target_half[half_pick]
        row_lse = sweep(cost_grid_t, target_here)
        row_back = a2a(row_lse)
        maxima, totals = combine_by(row_back, source_of_owner, blocks)
        other_maxima, other_totals = swap_rep((maxima, totals))
        merged = jnp.maximum(maxima, other_maxima)
        merged_totals = totals * jnp.exp(maxima - merged) + other_totals * jnp.exp(
            other_maxima - merged
        )
        source_lse = merged + jnp.log(merged_totals)
        source_dual = -EPSILON * source_lse
        sent_duals = jnp.where(served[:, None], -source_lse[source_index], 0.0)
        source_here = a2a(sent_duals)
        column_lse = sweep(cost_grid, source_here)
        col_max, col_tot = combine_by(column_lse, half_key, half_blocks)
        target_lse = col_max + jnp.log(col_tot)
        target_half = -target_lse

    target_here = target_half[half_pick]
    gradient_mine = gradient_sums(
        half_key, rep_index.reshape(1), cost_grid_t, source_here, target_here, received, own_half
    )
    gradient_half = lax.dynamic_slice_in_dim(gradient_mine, lower_block, half_blocks, 0)
    target_dual = both_halves(-EPSILON * target_lse, rep_index)
    gradient_other = lax.ppermute(gradient_half, "rep", [(0, 1), (1, 0)])
    gradient = lax.dynamic_update_slice_in_dim(
        gradient_mine, gradient_other, (1 - rep_index) * half_blocks, 0
    )
    return (
        source_dual.reshape(-1),
        target_dual.reshape(-1),
        gradient.reshape(blocks * block_len, feat_width),
    )


def solution(mesh):
    return jax.shard_map(
        on_device,
        mesh=mesh,
        in_specs=(
            P("pts", None),
            P("pts", None),
            P(("pts", "rep")),
            P(("pts", "rep")),
            P(("pts", "rep")),
        ),
        out_specs=(P("pts"), P("pts"), P("pts", None)),
        check_vma=False,
    )
```

```python
import jax
import jax.numpy as jnp
from jax import lax
from jax.experimental import pallas as pl
from jax.experimental.pallas import tpu as pltpu
from jax.sharding import PartitionSpec as P

BLOCK = 128
ITERS = 3


EPSILON = 0.05
NEG_BIG = -1e30
INV_EPS = 1.0 / EPSILON
SWEEP_STEP = 64
GRADIENT_STEP = 32
FIRST_STEP = 16


def columns_of(duals, step):
    pairs, side = duals.shape
    shaped = duals.reshape(pairs // step, step, side).transpose(0, 2, 1)
    return jnp.pad(shaped, ((0, 0), (0, 0), (0, side - step)))


def sweep_kernel(grid_ref, dual_ref, out_ref):
    side = grid_ref.shape[1]
    dual_cols = dual_ref[0]
    for p in range(grid_ref.shape[0]):
        dual_col = jnp.broadcast_to(dual_cols[:, p : p + 1], (side, side))
        scores = (dual_col - grid_ref[p]) * INV_EPS
        peak = jnp.max(scores, axis=0, keepdims=True)
        mass = jnp.sum(jnp.exp(scores - peak), axis=0, keepdims=True)
        out_ref[p : p + 1, :] = peak + jnp.log(mass)


def sweep(grids, duals):
    pairs, side, _ = grids.shape
    return pl.pallas_call(
        sweep_kernel,
        grid=(pairs // SWEEP_STEP,),
        in_specs=[
            pl.BlockSpec((SWEEP_STEP, side, side), lambda s: (s, 0, 0)),
            pl.BlockSpec((1, side, side), lambda s: (s, 0, 0)),
        ],
        out_specs=pl.BlockSpec((SWEEP_STEP, side), lambda s: (s, 0)),
        out_shape=jax.ShapeDtypeStruct((pairs, side), jnp.float32),
        cost_estimate=pl.CostEstimate(
            flops=8 * pairs * side * side,
            transcendentals=pairs * side * side,
            bytes_accessed=4 * pairs * side * (side + 2),
        ),
    )(grids, columns_of(duals, SWEEP_STEP))


def first_sweep_kernel(keys_ref, rows_ref, rows_sq_ref, half_ref, half_sq_ref, grid_t_ref, out_ref):
    step = pl.program_id(0)
    scale = 1.0 / rows_ref.shape[2]
    for p in range(rows_ref.shape[0]):
        key = keys_ref[step * FIRST_STEP + p]
        inner_dot_t = lax.dot_general(
            half_ref[key], rows_ref[p], (((1,), (1,)), ((), ())), preferred_element_type=jnp.float32
        )
        grid_t = (rows_sq_ref[p : p + 1, :] + half_sq_ref[key] - 2.0 * inner_dot_t) * scale
        grid_t_ref[p] = grid_t
        scores = -grid_t * INV_EPS
        peak = jnp.max(scores, axis=0, keepdims=True)
        mass = jnp.sum(jnp.exp(scores - peak), axis=0, keepdims=True)
        out_ref[p : p + 1, :] = peak + jnp.log(mass)


def first_sweep(keys, rows, rows_sq, half_targets):
    pairs, side, width = rows.shape
    half = half_targets.shape[0]
    half_sq = jnp.broadcast_to(squares(half_targets)[:, :, None], (half, side, side))
    return pl.pallas_call(
        first_sweep_kernel,
        grid_spec=pltpu.PrefetchScalarGridSpec(
            num_scalar_prefetch=1,
            grid=(pairs // FIRST_STEP,),
            in_specs=[
                pl.BlockSpec((FIRST_STEP, side, width), lambda s, k: (s, 0, 0)),
                pl.BlockSpec((FIRST_STEP, side), lambda s, k: (s, 0)),
                pl.BlockSpec((half, side, width), lambda s, k: (0, 0, 0)),
                pl.BlockSpec((half, side, side), lambda s, k: (0, 0, 0)),
            ],
            out_specs=[
                pl.BlockSpec((FIRST_STEP, side, side), lambda s, k: (s, 0, 0)),
                pl.BlockSpec((FIRST_STEP, side), lambda s, k: (s, 0)),
            ],
        ),
        out_shape=[
            jax.ShapeDtypeStruct((pairs, side, side), jnp.float32),
            jax.ShapeDtypeStruct((pairs, side), jnp.float32),
        ],
        cost_estimate=pl.CostEstimate(
            flops=2 * pairs * side * side * width + 10 * pairs * side * side,
            transcendentals=pairs * side * side,
            bytes_accessed=pairs * side * (2 * width + 4 * side + 8),
        ),
    )(keys, rows, rows_sq, half_targets, half_sq)


def gradient_kernel(
    keys_ref, grid_t_ref, source_ref, target_ref, rows_ref, half_ref, out_ref, mass_ref
):
    step = pl.program_id(0)
    side = grid_t_ref.shape[1]

    @pl.when(step == 0)
    def _():
        out_ref[...] = jnp.zeros_like(out_ref)
        mass_ref[...] = jnp.zeros_like(mass_ref)

    target_cols = target_ref[0]
    ones = jnp.ones((side, side), jnp.bfloat16)
    for p in range(grid_t_ref.shape[0]):
        key = keys_ref[step * GRADIENT_STEP + p]
        slot = jnp.maximum(key, 0)
        target_col = jnp.broadcast_to(target_cols[:, p : p + 1], (side, side))
        plan_t = jnp.exp((source_ref[p : p + 1, :] + target_col - grid_t_ref[p]) * INV_EPS)
        plan_t = jnp.where(key >= 0, plan_t, 0.0)
        weights = plan_t.astype(jnp.bfloat16)
        remainder = (plan_t - weights.astype(jnp.float32)).astype(jnp.bfloat16)
        mass = jnp.dot(weights, ones, preferred_element_type=jnp.float32) + jnp.dot(
            remainder, ones, preferred_element_type=jnp.float32
        )
        numerator = jnp.dot(weights, rows_ref[p], preferred_element_type=jnp.float32)
        out_ref[slot] -= numerator
        mass_ref[slot] += mass

    @pl.when(step == pl.num_programs(0) - 1)
    def _():
        mass = mass_ref[...]
        out_ref[...] += half_ref[...].astype(jnp.float32) * jnp.concatenate([mass, mass], axis=2)


def gradient_sums(keys, grids_t, source_duals, target_duals, rows, half_targets):
    pairs, side, _ = grids_t.shape
    width = rows.shape[2]
    half = half_targets.shape[0]
    return pl.pallas_call(
        gradient_kernel,
        grid_spec=pltpu.PrefetchScalarGridSpec(
            num_scalar_prefetch=1,
            grid=(pairs // GRADIENT_STEP,),
            in_specs=[
                pl.BlockSpec((GRADIENT_STEP, side, side), lambda s, k: (s, 0, 0)),
                pl.BlockSpec((GRADIENT_STEP, side), lambda s, k: (s, 0)),
                pl.BlockSpec((1, side, side), lambda s, k: (s, 0, 0)),
                pl.BlockSpec((GRADIENT_STEP, side, width), lambda s, k: (s, 0, 0)),
                pl.BlockSpec((half, side, width), lambda s, k: (0, 0, 0)),
            ],
            out_specs=pl.BlockSpec((half, side, width), lambda s, k: (0, 0, 0)),
            scratch_shapes=[pltpu.VMEM((half, side, side), jnp.float32)],
        ),
        out_shape=jax.ShapeDtypeStruct((half, side, width), jnp.float32),
        compiler_params=pltpu.CompilerParams(dimension_semantics=("arbitrary",)),
        cost_estimate=pl.CostEstimate(
            flops=2 * pairs * side * side * width + 8 * pairs * side * side,
            transcendentals=pairs * side * side,
            bytes_accessed=pairs * side * (4 * side + 2 * width) + half * side * width * 6,
        ),
    )(keys, grids_t, source_duals, columns_of(target_duals, GRADIENT_STEP), rows, half_targets)


def both_halves(mine, rep_index):
    other = lax.ppermute(mine, "rep", [(0, 1), (1, 0)])
    return jnp.where(
        rep_index == 0,
        jnp.concatenate([mine, other], axis=0),
        jnp.concatenate([other, mine], axis=0),
    )


def squares(blocks_in):
    return jnp.sum(jnp.square(blocks_in.astype(jnp.float32)), axis=-1)


def pair_costs(source_rows, target_rows, source_sq, target_sq):
    inner_dot = jnp.einsum(
        "gid,gjd->gij", source_rows, target_rows, preferred_element_type=jnp.float32
    )
    width = source_rows.shape[2]
    grid = (source_sq[:, :, None] + target_sq[:, None, :] - 2.0 * inner_dot) / width
    return grid


def pair_lse(scores, axis):
    peaks = jnp.max(scores, axis=axis)
    masses = jnp.sum(jnp.exp(scores - jnp.expand_dims(peaks, axis)), axis=axis)
    return peaks + jnp.log(masses)


def combine_by(values, block_key, key_count):
    member = (block_key[:, None] == jnp.arange(key_count)[None, :])[:, :, None]
    maxima = jnp.max(jnp.where(member, values[:, None, :], NEG_BIG), axis=0)
    shifts = jnp.where(member, values[:, None, :] - maxima[None, :, :], NEG_BIG)
    totals = jnp.sum(jnp.where(member, jnp.exp(shifts), 0.0), axis=0)
    return maxima, totals


def swap_rep(value):
    return lax.ppermute(value, "rep", [(0, 1), (1, 0)])


def a2a(value):
    return lax.all_to_all(value, "pts", split_axis=0, concat_axis=0, tiled=True)


def on_device(src_points, tgt_points, pair_source, pair_target, pair_count):
    peer_count = lax.axis_size("pts")
    point_rows, feat_width = src_points.shape
    block_len = BLOCK
    blocks = point_rows // block_len
    half_blocks = blocks // lax.axis_size("rep")
    rep_index = lax.axis_index("rep")
    lower_block = rep_index * half_blocks
    own_sources = src_points.reshape(blocks, block_len, feat_width)
    own_targets = tgt_points.reshape(blocks, block_len, feat_width)

    pair_total = pair_count[0]
    slot_total = pair_source.shape[0]
    usable = jnp.arange(slot_total) < pair_total
    source_local = jnp.where(usable, pair_source % blocks, 0)
    owner_ids = jnp.where(usable, pair_target // blocks, 0)
    target_local = jnp.where(usable, pair_target % blocks, 0)
    matched = (owner_ids[:, None] == jnp.arange(peer_count)[None, :]) & usable[:, None]
    wanted = jnp.max(jnp.where(matched, target_local[:, None], -1), axis=0)
    source_of_owner = jnp.max(jnp.where(matched, source_local[:, None], -1), axis=0)
    served = source_of_owner >= 0
    source_index = jnp.maximum(source_of_owner, 0)
    outgoing = own_sources[source_index]
    asked_info = jnp.stack(
        [
            squares(own_sources)[source_index],
            jnp.broadcast_to(wanted.astype(jnp.float32)[:, None], (peer_count, block_len)),
        ],
        axis=1,
    )
    asked_info = a2a(asked_info)
    received = a2a(outgoing)
    asked_ids = asked_info[:, 1, 0].astype(jnp.int32)
    received_sq = asked_info[:, 0, :]

    valid = asked_ids >= 0
    half_key = jnp.where(valid, asked_ids - lower_block, -1)
    half_pick = jnp.clip(half_key, 0, half_blocks - 1)
    own_half = lax.dynamic_slice_in_dim(own_targets, lower_block, half_blocks, 0)
    pair_targets = own_half[half_pick]
    target_sq = squares(own_half)[half_pick]
    cost_grid_t, first_row_lse = first_sweep(half_pick, received, received_sq, own_half)
    cost_grid = pair_costs(received, pair_targets, received_sq, target_sq)

    target_half = jnp.zeros((half_blocks, block_len), jnp.float32)
    for round_no in range(ITERS):
        target_here = target_half[half_pick]
        row_lse = first_row_lse if round_no == 0 else sweep(cost_grid_t, target_here)
        row_back = a2a(row_lse)
        maxima, totals = combine_by(row_back, source_of_owner, blocks)
        other_maxima, other_totals = swap_rep((maxima, totals))
        merged = jnp.maximum(maxima, other_maxima)
        merged_totals = totals * jnp.exp(maxima - merged) + other_totals * jnp.exp(
            other_maxima - merged
        )
        source_dual = -EPSILON * (merged + jnp.log(merged_totals))
        sent_duals = jnp.where(served[:, None], source_dual[source_index], 0.0)
        source_here = a2a(sent_duals)
        column_lse = sweep(cost_grid, source_here)
        col_max, col_tot = combine_by(column_lse, half_key, half_blocks)
        target_half = -EPSILON * (col_max + jnp.log(col_tot))

    target_here = target_half[half_pick]
    gradient_half = gradient_sums(
        half_key, cost_grid_t, source_here, target_here, received, own_half
    )
    target_dual = both_halves(target_half, rep_index)
    gradient = both_halves(gradient_half, rep_index)
    return (
        source_dual.reshape(-1),
        target_dual.reshape(-1),
        gradient.reshape(blocks * block_len, feat_width),
    )


def solution(mesh):
    return jax.shard_map(
        on_device,
        mesh=mesh,
        in_specs=(
            P("pts", None),
            P("pts", None),
            P(("pts", "rep")),
            P(("pts", "rep")),
            P(("pts", "rep")),
        ),
        out_specs=(P("pts"), P("pts"), P("pts", None)),
        check_vma=False,
    )
```

```python
import jax
import jax.numpy as jnp
from jax import lax
from jax.experimental import pallas as pl
from jax.experimental.pallas import tpu as pltpu
from jax.sharding import PartitionSpec as P

BLOCK = 128
ITERS = 3


EPSILON = 0.05
NEG_BIG = -1e30
INV_EPS = 1.0 / EPSILON
SWEEP_STEP = 64
GRADIENT_STEP = 32
FIRST_STEP = 16


def columns_of(duals, step):
    pairs, side = duals.shape
    shaped = duals.reshape(pairs // step, step, side).transpose(0, 2, 1)
    return jnp.pad(shaped, ((0, 0), (0, 0), (0, side - step)))


def sweep_kernel(grid_ref, dual_ref, out_ref):
    side = grid_ref.shape[1]
    dual_cols = dual_ref[0]
    for p in range(grid_ref.shape[0]):
        dual_col = jnp.broadcast_to(dual_cols[:, p : p + 1], (side, side))
        scores = (dual_col - grid_ref[p]) * INV_EPS
        peak = jnp.max(scores, axis=0, keepdims=True)
        mass = jnp.sum(jnp.exp(scores - peak), axis=0, keepdims=True)
        out_ref[p : p + 1, :] = peak + jnp.log(mass)


def sweep(grids, duals):
    pairs, side, _ = grids.shape
    return pl.pallas_call(
        sweep_kernel,
        grid=(pairs // SWEEP_STEP,),
        in_specs=[
            pl.BlockSpec((SWEEP_STEP, side, side), lambda s: (s, 0, 0)),
            pl.BlockSpec((1, side, side), lambda s: (s, 0, 0)),
        ],
        out_specs=pl.BlockSpec((SWEEP_STEP, side), lambda s: (s, 0)),
        out_shape=jax.ShapeDtypeStruct((pairs, side), jnp.float32),
        cost_estimate=pl.CostEstimate(
            flops=8 * pairs * side * side,
            transcendentals=pairs * side * side,
            bytes_accessed=4 * pairs * side * (side + 2),
        ),
    )(grids, columns_of(duals, SWEEP_STEP))


def first_sweep_kernel(keys_ref, rows_ref, rows_sq_ref, half_ref, half_sq_ref, grid_t_ref, out_ref):
    step = pl.program_id(0)
    scale = 1.0 / rows_ref.shape[2]
    for p in range(rows_ref.shape[0]):
        key = keys_ref[step * FIRST_STEP + p]
        inner_dot_t = lax.dot_general(
            half_ref[key], rows_ref[p], (((1,), (1,)), ((), ())), preferred_element_type=jnp.float32
        )
        grid_t = (rows_sq_ref[p : p + 1, :] + half_sq_ref[key] - 2.0 * inner_dot_t) * scale
        grid_t_ref[p] = grid_t
        scores = -grid_t * INV_EPS
        peak = jnp.max(scores, axis=0, keepdims=True)
        mass = jnp.sum(jnp.exp(scores - peak), axis=0, keepdims=True)
        out_ref[p : p + 1, :] = peak + jnp.log(mass)


def first_sweep(keys, rows, rows_sq, half_targets):
    pairs, side, width = rows.shape
    half = half_targets.shape[0]
    half_sq = jnp.broadcast_to(squares(half_targets)[:, :, None], (half, side, side))
    return pl.pallas_call(
        first_sweep_kernel,
        grid_spec=pltpu.PrefetchScalarGridSpec(
            num_scalar_prefetch=1,
            grid=(pairs // FIRST_STEP,),
            in_specs=[
                pl.BlockSpec((FIRST_STEP, side, width), lambda s, k: (s, 0, 0)),
                pl.BlockSpec((FIRST_STEP, side), lambda s, k: (s, 0)),
                pl.BlockSpec((half, side, width), lambda s, k: (0, 0, 0)),
                pl.BlockSpec((half, side, side), lambda s, k: (0, 0, 0)),
            ],
            out_specs=[
                pl.BlockSpec((FIRST_STEP, side, side), lambda s, k: (s, 0, 0)),
                pl.BlockSpec((FIRST_STEP, side), lambda s, k: (s, 0)),
            ],
        ),
        out_shape=[
            jax.ShapeDtypeStruct((pairs, side, side), jnp.float32),
            jax.ShapeDtypeStruct((pairs, side), jnp.float32),
        ],
        cost_estimate=pl.CostEstimate(
            flops=2 * pairs * side * side * width + 10 * pairs * side * side,
            transcendentals=pairs * side * side,
            bytes_accessed=pairs * side * (2 * width + 4 * side + 8),
        ),
    )(keys, rows, rows_sq, half_targets, half_sq)


def gradient_kernel(
    keys_ref, grid_t_ref, source_ref, target_ref, rows_ref, half_ref, out_ref, mass_ref
):
    step = pl.program_id(0)
    side = grid_t_ref.shape[1]

    @pl.when(step == 0)
    def _():
        out_ref[...] = jnp.zeros_like(out_ref)
        mass_ref[...] = jnp.zeros_like(mass_ref)

    target_cols = target_ref[0]
    ones = jnp.ones((side, side), jnp.bfloat16)
    for p in range(grid_t_ref.shape[0]):
        key = keys_ref[step * GRADIENT_STEP + p]
        slot = jnp.maximum(key, 0)
        target_col = jnp.broadcast_to(target_cols[:, p : p + 1], (side, side))
        plan_t = jnp.exp((source_ref[p : p + 1, :] + target_col - grid_t_ref[p]) * INV_EPS)
        plan_t = jnp.where(key >= 0, plan_t, 0.0)
        weights = plan_t.astype(jnp.bfloat16)
        remainder = (plan_t - weights.astype(jnp.float32)).astype(jnp.bfloat16)
        mass = jnp.dot(weights, ones, preferred_element_type=jnp.float32) + jnp.dot(
            remainder, ones, preferred_element_type=jnp.float32
        )
        numerator = jnp.dot(weights, rows_ref[p], preferred_element_type=jnp.float32)
        out_ref[slot] -= numerator
        mass_ref[slot] += mass

    @pl.when(step == pl.num_programs(0) - 1)
    def _():
        mass = mass_ref[...]
        out_ref[...] += half_ref[...].astype(jnp.float32) * jnp.concatenate([mass, mass], axis=2)


def gradient_sums(keys, grids_t, source_duals, target_duals, rows, half_targets):
    pairs, side, _ = grids_t.shape
    width = rows.shape[2]
    half = half_targets.shape[0]
    return pl.pallas_call(
        gradient_kernel,
        grid_spec=pltpu.PrefetchScalarGridSpec(
            num_scalar_prefetch=1,
            grid=(pairs // GRADIENT_STEP,),
            in_specs=[
                pl.BlockSpec((GRADIENT_STEP, side, side), lambda s, k: (s, 0, 0)),
                pl.BlockSpec((GRADIENT_STEP, side), lambda s, k: (s, 0)),
                pl.BlockSpec((1, side, side), lambda s, k: (s, 0, 0)),
                pl.BlockSpec((GRADIENT_STEP, side, width), lambda s, k: (s, 0, 0)),
                pl.BlockSpec((half, side, width), lambda s, k: (0, 0, 0)),
            ],
            out_specs=pl.BlockSpec((half, side, width), lambda s, k: (0, 0, 0)),
            scratch_shapes=[pltpu.VMEM((half, side, side), jnp.float32)],
        ),
        out_shape=jax.ShapeDtypeStruct((half, side, width), jnp.float32),
        compiler_params=pltpu.CompilerParams(dimension_semantics=("arbitrary",)),
        cost_estimate=pl.CostEstimate(
            flops=2 * pairs * side * side * width + 8 * pairs * side * side,
            transcendentals=pairs * side * side,
            bytes_accessed=pairs * side * (4 * side + 2 * width) + half * side * width * 6,
        ),
    )(keys, grids_t, source_duals, columns_of(target_duals, GRADIENT_STEP), rows, half_targets)


def both_halves(mine, rep_index):
    other = lax.ppermute(mine, "rep", [(0, 1), (1, 0)])
    return jnp.where(
        rep_index == 0,
        jnp.concatenate([mine, other], axis=0),
        jnp.concatenate([other, mine], axis=0),
    )


def squares(blocks_in):
    return jnp.sum(jnp.square(blocks_in.astype(jnp.float32)), axis=-1)


def pair_costs(source_rows, target_rows, source_sq, target_sq):
    inner_dot = jnp.einsum(
        "gid,gjd->gij", source_rows, target_rows, preferred_element_type=jnp.float32
    )
    width = source_rows.shape[2]
    grid = (source_sq[:, :, None] + target_sq[:, None, :] - 2.0 * inner_dot) / width
    return grid


def pair_lse(scores, axis):
    peaks = jnp.max(scores, axis=axis)
    masses = jnp.sum(jnp.exp(scores - jnp.expand_dims(peaks, axis)), axis=axis)
    return peaks + jnp.log(masses)


def combine_by(values, block_key, key_count):
    member = (block_key[:, None] == jnp.arange(key_count)[None, :])[:, :, None]
    maxima = jnp.max(jnp.where(member, values[:, None, :], NEG_BIG), axis=0)
    shifts = jnp.where(member, values[:, None, :] - maxima[None, :, :], NEG_BIG)
    totals = jnp.sum(jnp.where(member, jnp.exp(shifts), 0.0), axis=0)
    return maxima, totals


def swap_rep(value):
    return lax.ppermute(value, "rep", [(0, 1), (1, 0)])


def a2a(value):
    return lax.all_to_all(value, "pts", split_axis=0, concat_axis=0, tiled=True)


def on_device(src_points, tgt_points, pair_source, pair_target, pair_count):
    peer_count = lax.axis_size("pts")
    point_rows, feat_width = src_points.shape
    block_len = BLOCK
    blocks = point_rows // block_len
    half_blocks = blocks // lax.axis_size("rep")
    rep_index = lax.axis_index("rep")
    lower_block = rep_index * half_blocks
    own_sources = src_points.reshape(blocks, block_len, feat_width)
    own_targets = tgt_points.reshape(blocks, block_len, feat_width)

    pair_total = pair_count[0]
    slot_total = pair_source.shape[0]
    usable = jnp.arange(slot_total) < pair_total
    source_local = jnp.where(usable, pair_source % blocks, 0)
    owner_ids = jnp.where(usable, pair_target // blocks, 0)
    target_local = jnp.where(usable, pair_target % blocks, 0)
    matched = (owner_ids[:, None] == jnp.arange(peer_count)[None, :]) & usable[:, None]
    wanted = jnp.max(jnp.where(matched, target_local[:, None], -1), axis=0)
    source_of_owner = jnp.max(jnp.where(matched, source_local[:, None], -1), axis=0)
    served = source_of_owner >= 0
    source_index = jnp.maximum(source_of_owner, 0)
    outgoing = own_sources[source_index]
    asked_info = jnp.stack(
        [
            squares(own_sources)[source_index],
            jnp.broadcast_to(wanted.astype(jnp.float32)[:, None], (peer_count, block_len)),
        ],
        axis=1,
    )
    asked_info = a2a(asked_info)
    received = a2a(outgoing)
    asked_ids = asked_info[:, 1, 0].astype(jnp.int32)
    received_sq = asked_info[:, 0, :]

    valid = asked_ids >= 0
    half_key = jnp.where(valid, asked_ids - lower_block, -1)
    half_pick = jnp.clip(half_key, 0, half_blocks - 1)
    own_half = lax.dynamic_slice_in_dim(own_targets, lower_block, half_blocks, 0)
    pair_targets = own_half[half_pick]
    target_sq = squares(own_half)[half_pick]
    cost_grid_t, first_row_lse = first_sweep(half_pick, received, received_sq, own_half)
    cost_grid = jnp.swapaxes(cost_grid_t, 1, 2)

    target_half = jnp.zeros((half_blocks, block_len), jnp.float32)
    for round_no in range(ITERS):
        target_here = target_half[half_pick]
        row_lse = first_row_lse if round_no == 0 else sweep(cost_grid_t, target_here)
        row_back = a2a(row_lse)
        maxima, totals = combine_by(row_back, source_of_owner, blocks)
        other_maxima, other_totals = swap_rep((maxima, totals))
        merged = jnp.maximum(maxima, other_maxima)
        merged_totals = totals * jnp.exp(maxima - merged) + other_totals * jnp.exp(
            other_maxima - merged
        )
        source_dual = -EPSILON * (merged + jnp.log(merged_totals))
        sent_duals = jnp.where(served[:, None], source_dual[source_index], 0.0)
        source_here = a2a(sent_duals)
        column_lse = sweep(cost_grid, source_here)
        col_max, col_tot = combine_by(column_lse, half_key, half_blocks)
        target_half = -EPSILON * (col_max + jnp.log(col_tot))

    target_here = target_half[half_pick]
    gradient_half = gradient_sums(
        half_key, cost_grid_t, source_here, target_here, received, own_half
    )
    target_dual = both_halves(target_half, rep_index)
    gradient = both_halves(gradient_half, rep_index)
    return (
        source_dual.reshape(-1),
        target_dual.reshape(-1),
        gradient.reshape(blocks * block_len, feat_width),
    )


def solution(mesh):
    return jax.shard_map(
        on_device,
        mesh=mesh,
        in_specs=(
            P("pts", None),
            P("pts", None),
            P(("pts", "rep")),
            P(("pts", "rep")),
            P(("pts", "rep")),
        ),
        out_specs=(P("pts"), P("pts"), P("pts", None)),
        check_vma=False,
    )
```

```python
import jax
import jax.numpy as jnp
from jax import lax
from jax.experimental import pallas as pl
from jax.experimental.pallas import tpu as pltpu
from jax.sharding import PartitionSpec as P

BLOCK = 128
ITERS = 3


EPSILON = 0.05
NEG_BIG = -1e30
INV_EPS = 1.0 / EPSILON
SWEEP_STEP = 64
GRADIENT_STEP = 64


def columns_of(duals, step):
    pairs, side = duals.shape
    shaped = duals.reshape(pairs // step, step, side).transpose(0, 2, 1)
    return jnp.pad(shaped, ((0, 0), (0, 0), (0, side - step)))


def sweep_kernel(grid_ref, dual_ref, out_ref):
    side = grid_ref.shape[1]
    dual_cols = dual_ref[0]
    for p in range(grid_ref.shape[0]):
        dual_col = jnp.broadcast_to(dual_cols[:, p : p + 1], (side, side))
        scores = (dual_col - grid_ref[p]) * INV_EPS
        peak = jnp.max(scores, axis=0, keepdims=True)
        mass = jnp.sum(jnp.exp(scores - peak), axis=0, keepdims=True)
        out_ref[p : p + 1, :] = peak + jnp.log(mass)


def sweep(grids, duals):
    pairs, side, _ = grids.shape
    return pl.pallas_call(
        sweep_kernel,
        grid=(pairs // SWEEP_STEP,),
        in_specs=[
            pl.BlockSpec((SWEEP_STEP, side, side), lambda s: (s, 0, 0)),
            pl.BlockSpec((1, side, side), lambda s: (s, 0, 0)),
        ],
        out_specs=pl.BlockSpec((SWEEP_STEP, side), lambda s: (s, 0)),
        out_shape=jax.ShapeDtypeStruct((pairs, side), jnp.float32),
        cost_estimate=pl.CostEstimate(
            flops=8 * pairs * side * side,
            transcendentals=pairs * side * side,
            bytes_accessed=4 * pairs * side * (side + 2),
        ),
    )(grids, columns_of(duals, SWEEP_STEP))


def gradient_kernel(
    keys_ref, grid_t_ref, source_ref, target_ref, rows_ref, half_ref, out_ref, mass_ref
):
    step = pl.program_id(0)
    side = grid_t_ref.shape[1]

    @pl.when(step == 0)
    def _():
        out_ref[...] = jnp.zeros_like(out_ref)
        mass_ref[...] = jnp.zeros_like(mass_ref)

    target_cols = target_ref[0]
    ones = jnp.ones((side, side), jnp.bfloat16)
    for p in range(grid_t_ref.shape[0]):
        key = keys_ref[step * GRADIENT_STEP + p]
        slot = jnp.maximum(key, 0)
        target_col = jnp.broadcast_to(target_cols[:, p : p + 1], (side, side))
        plan_t = jnp.exp((source_ref[p : p + 1, :] + target_col - grid_t_ref[p]) * INV_EPS)
        plan_t = jnp.where(key >= 0, plan_t, 0.0)
        weights = plan_t.astype(jnp.bfloat16)
        remainder = (plan_t - weights.astype(jnp.float32)).astype(jnp.bfloat16)
        mass = jnp.dot(weights, ones, preferred_element_type=jnp.float32) + jnp.dot(
            remainder, ones, preferred_element_type=jnp.float32
        )
        numerator = jnp.dot(weights, rows_ref[p], preferred_element_type=jnp.float32)
        out_ref[slot] -= numerator
        mass_ref[slot] += mass

    @pl.when(step == pl.num_programs(0) - 1)
    def _():
        mass = mass_ref[...]
        out_ref[...] += half_ref[...].astype(jnp.float32) * jnp.concatenate([mass, mass], axis=2)


def gradient_sums(keys, grids_t, source_duals, target_duals, rows, half_targets):
    pairs, side, _ = grids_t.shape
    width = rows.shape[2]
    half = half_targets.shape[0]
    return pl.pallas_call(
        gradient_kernel,
        grid_spec=pltpu.PrefetchScalarGridSpec(
            num_scalar_prefetch=1,
            grid=(pairs // GRADIENT_STEP,),
            in_specs=[
                pl.BlockSpec((GRADIENT_STEP, side, side), lambda s, k: (s, 0, 0)),
                pl.BlockSpec((GRADIENT_STEP, side), lambda s, k: (s, 0)),
                pl.BlockSpec((1, side, side), lambda s, k: (s, 0, 0)),
                pl.BlockSpec((GRADIENT_STEP, side, width), lambda s, k: (s, 0, 0)),
                pl.BlockSpec((half, side, width), lambda s, k: (0, 0, 0)),
            ],
            out_specs=pl.BlockSpec((half, side, width), lambda s, k: (0, 0, 0)),
            scratch_shapes=[pltpu.VMEM((half, side, side), jnp.float32)],
        ),
        out_shape=jax.ShapeDtypeStruct((half, side, width), jnp.float32),
        compiler_params=pltpu.CompilerParams(dimension_semantics=("arbitrary",)),
        cost_estimate=pl.CostEstimate(
            flops=2 * pairs * side * side * width + 8 * pairs * side * side,
            transcendentals=pairs * side * side,
            bytes_accessed=pairs * side * (4 * side + 2 * width) + half * side * width * 6,
        ),
    )(keys, grids_t, source_duals, columns_of(target_duals, GRADIENT_STEP), rows, half_targets)


def both_halves(mine, rep_index):
    other = lax.ppermute(mine, "rep", [(0, 1), (1, 0)])
    return jnp.where(
        rep_index == 0,
        jnp.concatenate([mine, other], axis=0),
        jnp.concatenate([other, mine], axis=0),
    )


def squares(blocks_in):
    return jnp.sum(jnp.square(blocks_in.astype(jnp.float32)), axis=-1)


def pair_costs(source_rows, target_rows, source_sq, target_sq):
    inner_dot = jnp.einsum(
        "gid,gjd->gij", source_rows, target_rows, preferred_element_type=jnp.float32
    )
    inner_dot_t = jnp.einsum(
        "gjd,gid->gji", target_rows, source_rows, preferred_element_type=jnp.float32
    )
    width = source_rows.shape[2]
    grid = (source_sq[:, :, None] + target_sq[:, None, :] - 2.0 * inner_dot) / width
    grid_t = (source_sq[:, None, :] + target_sq[:, :, None] - 2.0 * inner_dot_t) / width
    return grid, grid_t


def pair_lse(scores, axis):
    peaks = jnp.max(scores, axis=axis)
    masses = jnp.sum(jnp.exp(scores - jnp.expand_dims(peaks, axis)), axis=axis)
    return peaks + jnp.log(masses)


def combine_by(values, block_key, key_count):
    member = (block_key[:, None] == jnp.arange(key_count)[None, :])[:, :, None]
    maxima = jnp.max(jnp.where(member, values[:, None, :], NEG_BIG), axis=0)
    shifts = jnp.where(member, values[:, None, :] - maxima[None, :, :], NEG_BIG)
    totals = jnp.sum(jnp.where(member, jnp.exp(shifts), 0.0), axis=0)
    return maxima, totals


def swap_rep(value):
    return lax.ppermute(value, "rep", [(0, 1), (1, 0)])


def a2a(value):
    return lax.all_to_all(value, "pts", split_axis=0, concat_axis=0, tiled=True)


def on_device(src_points, tgt_points, pair_source, pair_target, pair_count):
    peer_count = lax.axis_size("pts")
    point_rows, feat_width = src_points.shape
    block_len = BLOCK
    blocks = point_rows // block_len
    half_blocks = blocks // lax.axis_size("rep")
    rep_index = lax.axis_index("rep")
    lower_block = rep_index * half_blocks
    own_sources = src_points.reshape(blocks, block_len, feat_width)
    own_targets = tgt_points.reshape(blocks, block_len, feat_width)

    pair_total = pair_count[0]
    slot_total = pair_source.shape[0]
    usable = jnp.arange(slot_total) < pair_total
    source_local = jnp.where(usable, pair_source % blocks, 0)
    owner_ids = jnp.where(usable, pair_target // blocks, 0)
    target_local = jnp.where(usable, pair_target % blocks, 0)
    matched = (owner_ids[:, None] == jnp.arange(peer_count)[None, :]) & usable[:, None]
    wanted = jnp.max(jnp.where(matched, target_local[:, None], -1), axis=0)
    source_of_owner = jnp.max(jnp.where(matched, source_local[:, None], -1), axis=0)
    served = source_of_owner >= 0
    source_index = jnp.maximum(source_of_owner, 0)
    outgoing = own_sources[source_index]
    asked_info = jnp.stack(
        [
            squares(own_sources)[source_index],
            jnp.broadcast_to(wanted.astype(jnp.float32)[:, None], (peer_count, block_len)),
        ],
        axis=1,
    )
    asked_info = a2a(asked_info)
    received = a2a(outgoing)
    asked_ids = asked_info[:, 1, 0].astype(jnp.int32)
    received_sq = asked_info[:, 0, :]

    valid = asked_ids >= 0
    half_key = jnp.where(valid, asked_ids - lower_block, -1)
    half_pick = jnp.clip(half_key, 0, half_blocks - 1)
    own_half = lax.dynamic_slice_in_dim(own_targets, lower_block, half_blocks, 0)
    pair_targets = own_half[half_pick]
    target_sq = squares(own_half)[half_pick]
    cost_grid, cost_grid_t = pair_costs(received, pair_targets, received_sq, target_sq)

    target_half = jnp.zeros((half_blocks, block_len), jnp.float32)
    for round_no in range(ITERS):
        target_here = target_half[half_pick]
        row_lse = sweep(cost_grid_t, target_here)
        row_back = a2a(row_lse)
        maxima, totals = combine_by(row_back, source_of_owner, blocks)
        other_maxima, other_totals = swap_rep((maxima, totals))
        merged = jnp.maximum(maxima, other_maxima)
        merged_totals = totals * jnp.exp(maxima - merged) + other_totals * jnp.exp(
            other_maxima - merged
        )
        source_dual = -EPSILON * (merged + jnp.log(merged_totals))
        sent_duals = jnp.where(served[:, None], source_dual[source_index], 0.0)
        source_here = a2a(sent_duals)
        column_lse = sweep(cost_grid, source_here)
        col_max, col_tot = combine_by(column_lse, half_key, half_blocks)
        target_half = -EPSILON * (col_max + jnp.log(col_tot))

    target_here = target_half[half_pick]
    gradient_half = gradient_sums(
        half_key, cost_grid_t, source_here, target_here, received, own_half
    )
    target_dual = both_halves(target_half, rep_index)
    gradient = both_halves(gradient_half, rep_index)
    return (
        source_dual.reshape(-1),
        target_dual.reshape(-1),
        gradient.reshape(blocks * block_len, feat_width),
    )


def solution(mesh):
    return jax.shard_map(
        on_device,
        mesh=mesh,
        in_specs=(
            P("pts", None),
            P("pts", None),
            P(("pts", "rep")),
            P(("pts", "rep")),
            P(("pts", "rep")),
        ),
        out_specs=(P("pts"), P("pts"), P("pts", None)),
        check_vma=False,
    )
```

```python
import jax
import jax.numpy as jnp
from jax import lax
from jax.experimental import pallas as pl
from jax.experimental.pallas import tpu as pltpu
from jax.sharding import PartitionSpec as P

BLOCK = 128
ITERS = 3


EPSILON = 0.05
NEG_BIG = -1e30
INV_EPS = 1.0 / EPSILON
SWEEP_STEP = 128
GRADIENT_STEP = 64


def columns_of(duals, step):
    pairs, side = duals.shape
    shaped = duals.reshape(pairs // step, step, side).transpose(0, 2, 1)
    return jnp.pad(shaped, ((0, 0), (0, 0), (0, side - step)))


def sweep_kernel(grid_ref, dual_ref, out_ref):
    side = grid_ref.shape[1]
    dual_cols = dual_ref[0]
    for p in range(grid_ref.shape[0]):
        dual_col = jnp.broadcast_to(dual_cols[:, p : p + 1], (side, side))
        scores = (dual_col - grid_ref[p]) * INV_EPS
        peak = jnp.max(scores, axis=0, keepdims=True)
        mass = jnp.sum(jnp.exp(scores - peak), axis=0, keepdims=True)
        out_ref[p : p + 1, :] = peak + jnp.log(mass)


def sweep(grids, duals):
    pairs, side, _ = grids.shape
    return pl.pallas_call(
        sweep_kernel,
        grid=(pairs // SWEEP_STEP,),
        in_specs=[
            pl.BlockSpec((SWEEP_STEP, side, side), lambda s: (s, 0, 0)),
            pl.BlockSpec((1, side, side), lambda s: (s, 0, 0)),
        ],
        out_specs=pl.BlockSpec((SWEEP_STEP, side), lambda s: (s, 0)),
        out_shape=jax.ShapeDtypeStruct((pairs, side), jnp.float32),
        cost_estimate=pl.CostEstimate(
            flops=8 * pairs * side * side,
            transcendentals=pairs * side * side,
            bytes_accessed=4 * pairs * side * (side + 2),
        ),
    )(grids, columns_of(duals, SWEEP_STEP))


def gradient_kernel(
    keys_ref, grid_t_ref, source_ref, target_ref, rows_ref, half_ref, out_ref, mass_ref
):
    step = pl.program_id(0)
    side = grid_t_ref.shape[1]

    @pl.when(step == 0)
    def _():
        out_ref[...] = jnp.zeros_like(out_ref)
        mass_ref[...] = jnp.zeros_like(mass_ref)

    target_cols = target_ref[0]
    ones = jnp.ones((side, side), jnp.bfloat16)
    for p in range(grid_t_ref.shape[0]):
        key = keys_ref[step * GRADIENT_STEP + p]
        slot = jnp.maximum(key, 0)
        target_col = jnp.broadcast_to(target_cols[:, p : p + 1], (side, side))
        plan_t = jnp.exp((source_ref[p : p + 1, :] + target_col - grid_t_ref[p]) * INV_EPS)
        plan_t = jnp.where(key >= 0, plan_t, 0.0)
        weights = plan_t.astype(jnp.bfloat16)
        remainder = (plan_t - weights.astype(jnp.float32)).astype(jnp.bfloat16)
        mass = jnp.dot(weights, ones, preferred_element_type=jnp.float32) + jnp.dot(
            remainder, ones, preferred_element_type=jnp.float32
        )
        numerator = jnp.dot(weights, rows_ref[p], preferred_element_type=jnp.float32)
        out_ref[slot] -= numerator
        mass_ref[slot] += mass

    @pl.when(step == pl.num_programs(0) - 1)
    def _():
        mass = mass_ref[...]
        out_ref[...] += half_ref[...].astype(jnp.float32) * jnp.concatenate([mass, mass], axis=2)


def gradient_sums(keys, grids_t, source_duals, target_duals, rows, half_targets):
    pairs, side, _ = grids_t.shape
    width = rows.shape[2]
    half = half_targets.shape[0]
    return pl.pallas_call(
        gradient_kernel,
        grid_spec=pltpu.PrefetchScalarGridSpec(
            num_scalar_prefetch=1,
            grid=(pairs // GRADIENT_STEP,),
            in_specs=[
                pl.BlockSpec((GRADIENT_STEP, side, side), lambda s, k: (s, 0, 0)),
                pl.BlockSpec((GRADIENT_STEP, side), lambda s, k: (s, 0)),
                pl.BlockSpec((1, side, side), lambda s, k: (s, 0, 0)),
                pl.BlockSpec((GRADIENT_STEP, side, width), lambda s, k: (s, 0, 0)),
                pl.BlockSpec((half, side, width), lambda s, k: (0, 0, 0)),
            ],
            out_specs=pl.BlockSpec((half, side, width), lambda s, k: (0, 0, 0)),
            scratch_shapes=[pltpu.VMEM((half, side, side), jnp.float32)],
        ),
        out_shape=jax.ShapeDtypeStruct((half, side, width), jnp.float32),
        compiler_params=pltpu.CompilerParams(dimension_semantics=("arbitrary",)),
        cost_estimate=pl.CostEstimate(
            flops=2 * pairs * side * side * width + 8 * pairs * side * side,
            transcendentals=pairs * side * side,
            bytes_accessed=pairs * side * (4 * side + 2 * width) + half * side * width * 6,
        ),
    )(keys, grids_t, source_duals, columns_of(target_duals, GRADIENT_STEP), rows, half_targets)


def both_halves(mine, rep_index):
    other = lax.ppermute(mine, "rep", [(0, 1), (1, 0)])
    return jnp.where(
        rep_index == 0,
        jnp.concatenate([mine, other], axis=0),
        jnp.concatenate([other, mine], axis=0),
    )


def squares(blocks_in):
    return jnp.sum(jnp.square(blocks_in.astype(jnp.float32)), axis=-1)


def pair_costs(source_rows, target_rows, source_sq, target_sq):
    inner_dot = jnp.einsum(
        "gid,gjd->gij", source_rows, target_rows, preferred_element_type=jnp.float32
    )
    inner_dot_t = jnp.einsum(
        "gjd,gid->gji", target_rows, source_rows, preferred_element_type=jnp.float32
    )
    width = source_rows.shape[2]
    grid = (source_sq[:, :, None] + target_sq[:, None, :] - 2.0 * inner_dot) / width
    grid_t = (source_sq[:, None, :] + target_sq[:, :, None] - 2.0 * inner_dot_t) / width
    return grid, grid_t


def pair_lse(scores, axis):
    peaks = jnp.max(scores, axis=axis)
    masses = jnp.sum(jnp.exp(scores - jnp.expand_dims(peaks, axis)), axis=axis)
    return peaks + jnp.log(masses)


def combine_by(values, block_key, key_count):
    member = (block_key[:, None] == jnp.arange(key_count)[None, :])[:, :, None]
    maxima = jnp.max(jnp.where(member, values[:, None, :], NEG_BIG), axis=0)
    shifts = jnp.where(member, values[:, None, :] - maxima[None, :, :], NEG_BIG)
    totals = jnp.sum(jnp.where(member, jnp.exp(shifts), 0.0), axis=0)
    return maxima, totals


def swap_rep(value):
    return lax.ppermute(value, "rep", [(0, 1), (1, 0)])


def a2a(value):
    return lax.all_to_all(value, "pts", split_axis=0, concat_axis=0, tiled=True)


def on_device(src_points, tgt_points, pair_source, pair_target, pair_count):
    peer_count = lax.axis_size("pts")
    point_rows, feat_width = src_points.shape
    block_len = BLOCK
    blocks = point_rows // block_len
    half_blocks = blocks // lax.axis_size("rep")
    rep_index = lax.axis_index("rep")
    lower_block = rep_index * half_blocks
    own_sources = src_points.reshape(blocks, block_len, feat_width)
    own_targets = tgt_points.reshape(blocks, block_len, feat_width)

    pair_total = pair_count[0]
    slot_total = pair_source.shape[0]
    usable = jnp.arange(slot_total) < pair_total
    source_local = jnp.where(usable, pair_source % blocks, 0)
    owner_ids = jnp.where(usable, pair_target // blocks, 0)
    target_local = jnp.where(usable, pair_target % blocks, 0)
    matched = (owner_ids[:, None] == jnp.arange(peer_count)[None, :]) & usable[:, None]
    wanted = jnp.max(jnp.where(matched, target_local[:, None], -1), axis=0)
    source_of_owner = jnp.max(jnp.where(matched, source_local[:, None], -1), axis=0)
    served = source_of_owner >= 0
    source_index = jnp.maximum(source_of_owner, 0)
    outgoing = own_sources[source_index]
    asked_info = jnp.stack(
        [
            squares(own_sources)[source_index],
            jnp.broadcast_to(wanted.astype(jnp.float32)[:, None], (peer_count, block_len)),
        ],
        axis=1,
    )
    asked_info = a2a(asked_info)
    received = a2a(outgoing)
    asked_ids = asked_info[:, 1, 0].astype(jnp.int32)
    received_sq = asked_info[:, 0, :]

    valid = asked_ids >= 0
    half_key = jnp.where(valid, asked_ids - lower_block, -1)
    half_pick = jnp.clip(half_key, 0, half_blocks - 1)
    own_half = lax.dynamic_slice_in_dim(own_targets, lower_block, half_blocks, 0)
    pair_targets = own_half[half_pick]
    target_sq = squares(own_half)[half_pick]
    cost_grid, cost_grid_t = pair_costs(received, pair_targets, received_sq, target_sq)

    target_half = jnp.zeros((half_blocks, block_len), jnp.float32)
    for round_no in range(ITERS):
        target_here = target_half[half_pick]
        row_lse = sweep(cost_grid_t, target_here)
        row_back = a2a(row_lse)
        maxima, totals = combine_by(row_back, source_of_owner, blocks)
        other_maxima, other_totals = swap_rep((maxima, totals))
        merged = jnp.maximum(maxima, other_maxima)
        merged_totals = totals * jnp.exp(maxima - merged) + other_totals * jnp.exp(
            other_maxima - merged
        )
        source_dual = -EPSILON * (merged + jnp.log(merged_totals))
        sent_duals = jnp.where(served[:, None], source_dual[source_index], 0.0)
        source_here = a2a(sent_duals)
        column_lse = sweep(cost_grid, source_here)
        col_max, col_tot = combine_by(column_lse, half_key, half_blocks)
        target_half = -EPSILON * (col_max + jnp.log(col_tot))

    target_here = target_half[half_pick]
    gradient_half = gradient_sums(
        half_key, cost_grid_t, source_here, target_here, received, own_half
    )
    target_dual = both_halves(target_half, rep_index)
    gradient = both_halves(gradient_half, rep_index)
    return (
        source_dual.reshape(-1),
        target_dual.reshape(-1),
        gradient.reshape(blocks * block_len, feat_width),
    )


def solution(mesh):
    return jax.shard_map(
        on_device,
        mesh=mesh,
        in_specs=(
            P("pts", None),
            P("pts", None),
            P(("pts", "rep")),
            P(("pts", "rep")),
            P(("pts", "rep")),
        ),
        out_specs=(P("pts"), P("pts"), P("pts", None)),
        check_vma=False,
    )
```
